32 devices in a mesh: group: 8 (over z, x), blk: 4 (over y, core).
Axes of the slice: x: 2, y: 2, z: 4, core: 2. Of those that a mesh axis runs over, the one named last changes fastest.
Arguments:
- sources: bfloat16 [32768, 512], P(('group', 'blk')), may hold values from -20 to 20
- targets: bfloat16 [256, 512], P(('group', 'blk')), may hold values from -20 to 20
- target_potential: bfloat16 [256], P(('group', 'blk')), may hold values from -1.5 to 1.5
- log_source_mass: float32 [32768], P(('group', 'blk')), may hold values from -3 to 0
- log_target_mass: float32 [256], P(('group', 'blk')), may hold values from -3 to 0
Outputs:
- source_potential: float32 [32768], P(('group', 'blk'))
- target_update: float32 [256], P(('group', 'blk'))
The draws below stay inside these ranges and needn't reach their ends.
All inputs are finite; a program needn't handle non-finite values.
Results may differ from the reference program's by a relative error of at most 0.0003.
Values may be sent and summed in bfloat16 or wider, within the bound.
No kernel may reach another device: no remote copies, remote signals or barrier semaphores. Data moves between devices by JAX's collectives and lax.ppermute only.
A program may use at most 64 MiB of HBM per device.

```python
import jax
import jax.numpy as jnp
from jax import lax

D = 512
SRC_DEV = 1024
NSRC = 32768
NTGT = 256


def pair_base(key):
    base_key = jax.random.fold_in(key, 7)
    key_targets, key_sources = jax.random.split(base_key, 2)
    target_rows = jax.random.normal(key_targets, (NTGT, D), jnp.float32)
    source_rows = jax.random.normal(key_sources, (NSRC, D), jnp.float32)
    return (jnp.clip(source_rows, -20.0, 20.0), jnp.clip(target_rows, -20.0, 20.0))


def draw_sources(key, part):
    return pair_base(key)[0].astype(jnp.bfloat16)


def draw_targets(key, part):
    return pair_base(key)[1].astype(jnp.bfloat16)


def block_scale(stream_key, dims, cuts, least, top_value):
    def one(dim, parts):
        heights = jax.random.uniform(jax.random.fold_in(jax.random.fold_in(stream_key, 6), dim), (parts,), jnp.float32, least / len(cuts), top_value / len(cuts))
        return jnp.repeat(jnp.exp(heights), dims[dim] // parts).reshape((-1,) + (1,) * (len(dims) - dim - 1))

    gain = one(*cuts[0])
    for cut in cuts[1:]:
        gain = gain * one(*cut)
    return gain


def bell_draw(stream_key, extent, width, bound, cuts=(), held_as=jnp.bfloat16):
    level = block_scale(stream_key, extent, cuts, -0.22, 0.18) if cuts else 1.0
    array = jax.random.normal(stream_key, extent, jnp.float32) * width * level
    return jnp.minimum(jnp.maximum(array, -bound), bound).astype(held_as)


def setup_inputs(seed: int = 0) -> dict:
    key_of = jax.random.split(jax.random.key(seed), 6)
    sources = draw_sources(jax.random.fold_in(key_of[5], 71), 0)
    targets = draw_targets(jax.random.fold_in(key_of[5], 71), 0)
    target_potential = bell_draw(key_of[2], (NTGT,), 0.25, 1.5, ((0, 32),))
    log_source_mass = jnp.clip(-3.0 + 3.0 * jax.random.uniform(key_of[3], (NSRC,), jnp.float32) ** block_scale(key_of[3], (NSRC,), ((0, 32),), -0.2, 0.2), -3.0, 0.0)
    log_target_mass = jnp.clip(-3.0 + 3.0 * jax.random.uniform(key_of[4], (NTGT,), jnp.float32) ** block_scale(key_of[4], (NTGT,), ((0, 32),), -0.2, 0.2), -3.0, 0.0)
    return dict(sources=sources, targets=targets, target_potential=target_potential, log_source_mass=log_source_mass, log_target_mass=log_target_mass)


epsilon = 0.05


def reference(sources, targets, target_potential, log_source_mass, log_target_mass):
    features = sources.shape[1]
    factor = 2.0 / (features * epsilon)
    pot_f32 = target_potential.astype(jnp.float32)
    offset = pot_f32 / epsilon - jnp.sum(jnp.square(targets.astype(jnp.float32)), 1) / (features * epsilon)
    blocks = sources.reshape(-1, SRC_DEV, features)
    masses = log_source_mass.reshape(-1, SRC_DEV)

    def advance(running, pieces):
        block_rows, mass_log = pieces
        products = lax.dot_general(block_rows, targets, (((1,), (1,)), ((), ())), preferred_element_type=jnp.float32)
        logits = products * factor + offset[None, :]
        row_max = jnp.max(logits, 1)
        row_lse = row_max + jnp.log(jnp.sum(jnp.exp(logits - row_max[:, None]), 1))
        source_dual = mass_log - row_lse
        columns = logits - pot_f32[None, :] / epsilon + source_dual[:, None]
        col_max = jnp.max(columns, 0)
        col_sum = jnp.sum(jnp.exp(columns - col_max[None, :]), 0)
        old_max, old_sum = running
        new_max = jnp.maximum(old_max, col_max)
        new_sum = old_sum * jnp.exp(old_max - new_max) + col_sum * jnp.exp(col_max - new_max)
        return (new_max, new_sum), source_dual

    initial = (jnp.full((NTGT,), -1e30, jnp.float32), jnp.zeros((NTGT,), jnp.float32))
    (col_max, col_sum), source_dual = lax.scan(advance, initial, (blocks, masses))
    source_dual = source_dual.reshape(-1)
    source_potential = epsilon * source_dual + jnp.sum(jnp.square(sources.astype(jnp.float32)), 1) / features
    target_update = epsilon * (log_target_mass - (col_max + jnp.log(col_sum)))
    return (source_potential, target_update)
```

```python
import jax
import jax.numpy as jnp
from jax import lax
from jax.sharding import PartitionSpec as P

epsilon = 0.05
AXES = ("group", "blk")


def exchange(x, bit, count):
    route = [(i, i ^ (1 << bit)) for i in range(count)]
    return lax.ppermute(x, AXES, route)


def combine(first, second):
    new_max = jnp.maximum(first[0], second[0])
    new_sum = first[1] * jnp.exp(first[0] - new_max) + second[1] * jnp.exp(second[0] - new_max)
    return jnp.stack([new_max, new_sum])


def per_device(sources, targets, target_potential, log_source_mass, log_target_mass):
    count = lax.axis_size("group") * lax.axis_size("blk")
    levels = count.bit_length() - 1
    if (1 << levels) != count:
        raise ValueError("count not pow2")
    order = list(reversed(range(levels)))
    features = sources.shape[1]
    factor = 2.0 / (features * epsilon)

    held_rows, held_pots = targets, target_potential
    for bit in order:
        other_rows, other_pots = exchange((held_rows, held_pots), bit, count)
        held_rows = jnp.concatenate([held_rows, other_rows], 0)
        held_pots = jnp.concatenate([held_pots, other_pots], 0)

    pot_f32 = held_pots.astype(jnp.float32)
    offset = pot_f32 / epsilon - jnp.sum(jnp.square(held_rows.astype(jnp.float32)), 1) / (
        features * epsilon
    )
    products = lax.dot_general(
        sources, held_rows, (((1,), (1,)), ((), ())), preferred_element_type=jnp.float32
    )
    logits = products * factor + offset[None, :]
    row_max = jnp.max(logits, 1)
    row_lse = row_max + jnp.log(jnp.sum(jnp.exp(logits - row_max[:, None]), 1))
    source_dual = log_source_mass - row_lse
    columns = logits - pot_f32[None, :] / epsilon + source_dual[:, None]
    col_max = jnp.max(columns, 0)
    col_sum = jnp.sum(jnp.exp(columns - col_max[None, :]), 0)

    part = jnp.stack([col_max, col_sum])
    for bit in reversed(order):
        half = part.shape[1] // 2
        arrived = exchange(part[:, half:], bit, count)
        part = combine(part[:, :half], arrived)

    source_potential = epsilon * source_dual + jnp.sum(
        jnp.square(sources.astype(jnp.float32)), 1
    ) / features
    target_update = epsilon * (log_target_mass - (part[0] + jnp.log(part[1])))
    return (source_potential, target_update)


def solution(mesh):
    return jax.shard_map(
        per_device,
        mesh=mesh,
        in_specs=(
            P(AXES, None),
            P(AXES, None),
            P(AXES),
            P(AXES),
            P(AXES),
        ),
        out_specs=(P(AXES), P(AXES)),
        check_vma=False,
    )
```

```python
import jax
import jax.numpy as jnp
from jax import lax
from jax.sharding import PartitionSpec as P

epsilon = 0.05
AXES = ("group", "blk")


def exchange(x, bit, count):
    route = [(i, i ^ (1 << bit)) for i in range(count)]
    return lax.ppermute(x, AXES, route)


def combine(first, second):
    new_max = jnp.maximum(first[0], second[0])
    new_sum = first[1] * jnp.exp(first[0] - new_max) + second[1] * jnp.exp(second[0] - new_max)
    return jnp.stack([new_max, new_sum])


def per_device(sources, targets, target_potential, log_source_mass, log_target_mass):
    count = lax.axis_size("group") * lax.axis_size("blk")
    levels = count.bit_length() - 1
    if (1 << levels) != count:
        raise ValueError("count not pow2")
    order = list(reversed(range(levels)))
    features = sources.shape[1]
    factor = 2.0 / (features * epsilon)

    held = jnp.concatenate(
        [targets, jnp.broadcast_to(target_potential[:, None], (targets.shape[0], 128))], 1
    )
    for bit in order:
        held = jnp.concatenate([held, exchange(held, bit, count)], 0)
    held_rows, held_pots = held[:, :features], held[:, features]

    pot_f32 = held_pots.astype(jnp.float32)
    offset = pot_f32 / epsilon - jnp.sum(jnp.square(held_rows.astype(jnp.float32)), 1) / (
        features * epsilon
    )
    products = lax.dot_general(
        sources, held_rows, (((1,), (1,)), ((), ())), preferred_element_type=jnp.float32
    )
    logits = products * factor + offset[None, :]
    row_max = jnp.max(logits, 1)
    row_lse = row_max + jnp.log(jnp.sum(jnp.exp(logits - row_max[:, None]), 1))
    source_dual = log_source_mass - row_lse
    columns = logits - pot_f32[None, :] / epsilon + source_dual[:, None]
    col_max = jnp.max(columns, 0)
    col_sum = jnp.sum(jnp.exp(columns - col_max[None, :]), 0)

    part = jnp.stack([col_max, col_sum])
    for bit in reversed(order):
        half = part.shape[1] // 2
        arrived = exchange(part[:, half:], bit, count)
        part = combine(part[:, :half], arrived)

    source_potential = epsilon * source_dual + jnp.sum(
        jnp.square(sources.astype(jnp.float32)), 1
    ) / features
    target_update = epsilon * (log_target_mass - (part[0] + jnp.log(part[1])))
    return (source_potential, target_update)


def solution(mesh):
    return jax.shard_map(
        per_device,
        mesh=mesh,
        in_specs=(
            P(AXES, None),
            P(AXES, None),
            P(AXES),
            P(AXES),
            P(AXES),
        ),
        out_specs=(P(AXES), P(AXES)),
        check_vma=False,
    )
```

```python
import jax
import jax.numpy as jnp
from jax import lax
from jax.sharding import PartitionSpec as P

epsilon = 0.05
AXES = ("group", "blk")


def exchange(x, bit, count):
    route = [(i, i ^ (1 << bit)) for i in range(count)]
    return lax.ppermute(x, AXES, route)


def per_device(sources, targets, target_potential, log_source_mass, log_target_mass):
    count = lax.axis_size("group") * lax.axis_size("blk")
    levels = count.bit_length() - 1
    if (1 << levels) != count:
        raise ValueError("count not pow2")
    order = list(reversed(range(levels)))
    features = sources.shape[1]
    factor = 2.0 / (features * epsilon)

    held = lax.optimization_barrier(
        jnp.concatenate(
            [targets, jnp.broadcast_to(target_potential[:, None], (targets.shape[0], 128))], 1
        )
    )
    for bit in order:
        held = jnp.concatenate([held, exchange(held, bit, count)], 0)
    held_rows, held_pots = held[:, :features], held[:, features]

    pot_f32 = held_pots.astype(jnp.float32)
    offset = pot_f32 / epsilon - jnp.sum(jnp.square(held_rows.astype(jnp.float32)), 1) / (
        features * epsilon
    )
    products = lax.dot_general(
        sources, held_rows, (((1,), (1,)), ((), ())), preferred_element_type=jnp.float32
    )
    logits = products * factor + offset[None, :]
    row_max = jnp.max(logits, 1)
    row_lse = row_max + jnp.log(jnp.sum(jnp.exp(logits - row_max[:, None]), 1))
    source_dual = log_source_mass - row_lse
    columns = logits - pot_f32[None, :] / epsilon + source_dual[:, None]
    col_max = jnp.max(columns, 0)
    col_sum = jnp.sum(jnp.exp(columns - col_max[None, :]), 0)

    me = lax.axis_index(AXES)
    apart = me ^ jnp.arange(count)
    where = sum(((apart >> bit) & 1) << step for step, bit in enumerate(order))
    part = jnp.stack([col_max, col_sum]).reshape(2, count, -1)
    part = jnp.take(part, where, axis=1)
    part = lax.all_to_all(part, AXES, 1, 1, tiled=True)
    owned_max = jnp.max(part[0], 0)
    owned_sum = jnp.sum(part[1] * jnp.exp(part[0] - owned_max[None, :]), 0)
    part = (owned_max, owned_sum)

    source_potential = epsilon * source_dual + jnp.sum(
        jnp.square(sources.astype(jnp.float32)), 1
    ) / features
    target_update = epsilon * (log_target_mass - (part[0] + jnp.log(part[1])))
    return (source_potential, target_update)


def solution(mesh):
    return jax.shard_map(
        per_device,
        mesh=mesh,
        in_specs=(
            P(AXES, None),
            P(AXES, None),
            P(AXES),
            P(AXES),
            P(AXES),
        ),
        out_specs=(P(AXES), P(AXES)),
        check_vma=False,
    )
```

```python
import jax
import jax.numpy as jnp
from jax import lax
from jax.sharding import PartitionSpec as P

epsilon = 0.05
AXES = ("group", "blk")


def exchange(x, bit, count):
    route = [(i, i ^ (1 << bit)) for i in range(count)]
    return lax.ppermute(x, AXES, route)


def per_device(sources, targets, target_potential, log_source_mass, log_target_mass):
    count = lax.axis_size("group") * lax.axis_size("blk")
    levels = count.bit_length() - 1
    if (1 << levels) != count:
        raise ValueError("count not pow2")
    order = list(reversed(range(levels)))
    features = sources.shape[1]
    factor = 2.0 / (features * epsilon)

    lanes = jnp.broadcast_to(target_potential.astype(jnp.float32)[:, None], (targets.shape[0], 128))
    held = lax.optimization_barrier(
        jnp.concatenate([targets.astype(jnp.float32), lanes], 1).astype(jnp.bfloat16)
    )
    source_terms = lax.optimization_barrier(
        jnp.stack(
            [
                jnp.sum(jnp.square(sources.astype(jnp.float32)), 1) / features,
                log_source_mass,
            ]
        )
    )
    for bit in order:
        held = jnp.concatenate([held, exchange(held, bit, count)], 0)
    held_rows, held_pots = held[:, :features], held[:, features]

    pot_f32 = held_pots.astype(jnp.float32)
    offset = pot_f32 / epsilon - jnp.sum(jnp.square(held_rows.astype(jnp.float32)), 1) / (
        features * epsilon
    )
    products = lax.dot_general(
        sources, held_rows, (((1,), (1,)), ((), ())), preferred_element_type=jnp.float32
    )
    logits = products * factor + offset[None, :]
    row_max = jnp.max(logits, 1)
    row_lse = row_max + jnp.log(jnp.sum(jnp.exp(logits - row_max[:, None]), 1))
    source_dual = source_terms[1] - row_lse
    columns = logits - pot_f32[None, :] / epsilon + source_dual[:, None]
    col_max = jnp.max(columns, 0)
    col_sum = jnp.sum(jnp.exp(columns - col_max[None, :]), 0)

    me = lax.axis_index(AXES)
    apart = me ^ jnp.arange(count)
    where = sum(((apart >> bit) & 1) << step for step, bit in enumerate(order))
    choose = (where[:, None] == jnp.arange(count)[None, :]).astype(jnp.float32)
    part = jnp.stack([col_max.reshape(count, -1), col_sum.reshape(count, -1)], 1)
    part = jnp.dot(
        choose, part.reshape(count, -1), precision=lax.Precision.HIGHEST
    ).reshape(count, 2, -1)
    part = lax.all_to_all(part, AXES, 0, 0, tiled=True)
    owned_max = jnp.max(part[:, 0], 0)
    owned_sum = jnp.sum(part[:, 1] * jnp.exp(part[:, 0] - owned_max[None, :]), 0)
    part = (owned_max, owned_sum)

    source_potential = epsilon * source_dual + source_terms[0]
    target_update = epsilon * (log_target_mass - (part[0] + jnp.log(part[1])))
    return (source_potential, target_update)


def solution(mesh):
    return jax.shard_map(
        per_device,
        mesh=mesh,
        in_specs=(
            P(AXES, None),
            P(AXES, None),
            P(AXES),
            P(AXES),
            P(AXES),
        ),
        out_specs=(P(AXES), P(AXES)),
        check_vma=False,
    )
```

```python
import jax
import jax.numpy as jnp
from jax import lax
from jax.sharding import PartitionSpec as P

epsilon = 0.05
AXES = ("group", "blk")


def exchange(x, bit, count):
    route = [(i, i ^ (1 << bit)) for i in range(count)]
    return lax.ppermute(x, AXES, route)


def per_device(sources, targets, target_potential, log_source_mass, log_target_mass):
    count = lax.axis_size("group") * lax.axis_size("blk")
    levels = count.bit_length() - 1
    if (1 << levels) != count:
        raise ValueError("count not pow2")
    order = list(reversed(range(levels)))
    features = sources.shape[1]
    factor = 2.0 / (features * epsilon)

    lane = lax.broadcasted_iota(jnp.int32, (targets.shape[0], features + 128), 1)
    held = lax.optimization_barrier(
        jnp.where(
            lane < features,
            jnp.pad(targets, ((0, 0), (0, 128))),
            target_potential[:, None],
        )
    )
    source_terms = lax.optimization_barrier(
        jnp.stack(
            [
                jnp.sum(jnp.square(sources.astype(jnp.float32)), 1) / features,
                log_source_mass,
            ]
        )
    )
    for bit in order[:-1]:
        held = jnp.concatenate([held, exchange(held, bit, count)], 0)
    last = exchange(held, order[-1], count)

    def row_pass(block):
        pots = block[:, features].astype(jnp.float32)
        offset = pots / epsilon - jnp.sum(jnp.square(block[:, :features].astype(jnp.float32)), 1) / (
            features * epsilon
        )
        products = lax.dot_general(
            sources, block[:, :features], (((1,), (1,)), ((), ())),
            preferred_element_type=jnp.float32,
        )
        logits = products * factor + offset[None, :]
        block_max = jnp.max(logits, 1)
        return logits, pots, block_max, jnp.sum(jnp.exp(logits - block_max[:, None]), 1)

    first, second = row_pass(held), row_pass(last)
    row_max = jnp.maximum(first[2], second[2])
    row_lse = row_max + jnp.log(
        first[3] * jnp.exp(first[2] - row_max) + second[3] * jnp.exp(second[2] - row_max)
    )
    logits = jnp.concatenate([first[0], second[0]], 1)
    pot_f32 = jnp.concatenate([first[1], second[1]], 0)
    source_dual = source_terms[1] - row_lse
    columns = logits - pot_f32[None, :] / epsilon + source_dual[:, None]
    col_max = jnp.max(columns, 0)
    col_sum = jnp.sum(jnp.exp(columns - col_max[None, :]), 0)

    me = lax.axis_index(AXES)
    apart = me ^ jnp.arange(count)
    where = sum(((apart >> bit) & 1) << step for step, bit in enumerate(order))
    choose = (where[:, None] == jnp.arange(count)[None, :]).astype(jnp.float32)
    part = jnp.stack([col_max.reshape(count, -1), col_sum.reshape(count, -1)], 1)
    part = jnp.dot(
        choose, part.reshape(count, -1), precision=lax.Precision.HIGHEST
    ).reshape(count, 2, -1)
    part = lax.all_to_all(part, AXES, 0, 0, tiled=True)
    owned_max = jnp.max(part[:, 0], 0)
    owned_sum = jnp.sum(part[:, 1] * jnp.exp(part[:, 0] - owned_max[None, :]), 0)
    part = (owned_max, owned_sum)

    source_potential = epsilon * source_dual + source_terms[0]
    target_update = epsilon * (log_target_mass - (part[0] + jnp.log(part[1])))
    return (source_potential, target_update)


def solution(mesh):
    return jax.shard_map(
        per_device,
        mesh=mesh,
        in_specs=(
            P(AXES, None),
            P(AXES, None),
            P(AXES),
            P(AXES),
            P(AXES),
        ),
        out_specs=(P(AXES), P(AXES)),
        check_vma=False,
    )
```

```python
import functools

import jax
import jax.numpy as jnp
from jax import lax
from jax.sharding import PartitionSpec as P
from jax.experimental import pallas as pl
from jax.experimental.pallas import tpu as pltpu

epsilon = 0.05
AXES = ("group", "blk")


def exchange(x, bit, count):
    route = [(i, i ^ (1 << bit)) for i in range(count)]
    return lax.ppermute(x, AXES, route)


def tail(features, factor, src_ref, early_ref, last_ref, logits_ref, stats_ref, terms_ref,
         col_ref, pot_ref):
    block = last_ref[...]
    rows = block[:, :features]
    pots = block[:, features:features + 1].astype(jnp.float32)
    offset = pots / epsilon - jnp.sum(jnp.square(rows.astype(jnp.float32)), 1, keepdims=True) / (
        features * epsilon
    )
    late = lax.dot_general(
        rows, src_ref[...], (((1,), (1,)), ((), ())), preferred_element_type=jnp.float32
    ) * factor + offset
    late_max = jnp.max(late, 0, keepdims=True)
    late_sum = jnp.sum(jnp.exp(late - late_max), 0, keepdims=True)
    early_max = stats_ref[0:1, :]
    row_max = jnp.maximum(early_max, late_max)
    row_lse = row_max + jnp.log(
        stats_ref[1:2, :] * jnp.exp(early_max - row_max) + late_sum * jnp.exp(late_max - row_max)
    )
    dual = terms_ref[1:2, :] - row_lse
    pot_ref[...] = epsilon * dual + terms_ref[0:1, :]
    half = block.shape[0]
    for start, logits, block_pots in (
        (0, logits_ref[...], early_ref[:, features:features + 1].astype(jnp.float32)),
        (half, late, pots),
    ):
        column = logits - block_pots / epsilon + dual
        col_max = jnp.max(column, 1, keepdims=True)
        col_ref[start:start + half, 0:1] = col_max
        col_ref[start:start + half, 1:2] = jnp.sum(jnp.exp(column - col_max), 1, keepdims=True)

def per_device(sources, targets, target_potential, log_source_mass, log_target_mass):
    count = lax.axis_size("group") * lax.axis_size("blk")
    levels = count.bit_length() - 1
    if (1 << levels) != count:
        raise ValueError("count not pow2")
    order = list(reversed(range(levels)))
    features = sources.shape[1]
    factor = 2.0 / (features * epsilon)

    lane = lax.broadcasted_iota(jnp.int32, (targets.shape[0], features + 128), 1)
    held = lax.optimization_barrier(
        jnp.where(
            lane < features,
            jnp.pad(targets, ((0, 0), (0, 128))),
            target_potential[:, None],
        )
    )
    source_terms = lax.optimization_barrier(
        jnp.stack(
            [
                jnp.sum(jnp.square(sources.astype(jnp.float32)), 1) / features,
                log_source_mass,
            ]
        )
    )
    for bit in order[:-1]:
        held = jnp.concatenate([held, exchange(held, bit, count)], 0)
    last = exchange(held, order[-1], count)

    early_rows = held[:, :features]
    early_pots = held[:, features].astype(jnp.float32)
    early_offset = early_pots / epsilon - jnp.sum(
        jnp.square(early_rows.astype(jnp.float32)), 1
    ) / (features * epsilon)
    early_logits = lax.dot_general(
        early_rows, sources, (((1,), (1,)), ((), ())), preferred_element_type=jnp.float32
    ) * factor + early_offset[:, None]
    early_max = jnp.max(early_logits, 0)
    early_stats = jnp.stack([early_max, jnp.sum(jnp.exp(early_logits - early_max[None, :]), 0)])

    half = held.shape[0]
    vmem = pl.BlockSpec(memory_space=pltpu.VMEM)
    columns, source_potential = pl.pallas_call(
        functools.partial(tail, features, factor),
        out_shape=(
            jax.ShapeDtypeStruct((2 * half, 2), jnp.float32),
            jax.ShapeDtypeStruct((1, sources.shape[0]), jnp.float32),
        ),
        in_specs=[vmem] * 6,
        out_specs=(vmem, vmem),
        compiler_params=pltpu.CompilerParams(vmem_limit_bytes=24 * 1024 * 1024),
    )(sources, held, last, early_logits, early_stats, source_terms)
    source_potential = source_potential.reshape(-1)

    me = lax.axis_index(AXES)
    width = columns.shape[0] // count
    apart = me ^ (jnp.arange(count * width) // width)
    where = sum(((apart >> bit) & 1) << step for step, bit in enumerate(order))
    where = where * width + jnp.arange(count * width) % width
    choose = (where[:, None] == jnp.arange(count * width)[None, :]).astype(jnp.float32)
    part = jnp.dot(choose, columns, precision=lax.Precision.HIGHEST).reshape(count, width, 2)
    part = lax.all_to_all(part, AXES, 0, 0, tiled=True)
    owned_max = jnp.max(part[:, :, 0], 0)
    owned_sum = jnp.sum(part[:, :, 1] * jnp.exp(part[:, :, 0] - owned_max[None, :]), 0)
    part = (owned_max, owned_sum)

    target_update = epsilon * (log_target_mass - (part[0] + jnp.log(part[1])))
    return (source_potential, target_update)


def solution(mesh):
    return jax.shard_map(
        per_device,
        mesh=mesh,
        in_specs=(
            P(AXES, None),
            P(AXES, None),
            P(AXES),
            P(AXES),
            P(AXES),
        ),
        out_specs=(P(AXES), P(AXES)),
        check_vma=False,
    )
```

```python
import functools

import jax
import jax.numpy as jnp
from jax import lax
from jax.sharding import PartitionSpec as P
from jax.experimental import pallas as pl
from jax.experimental.pallas import tpu as pltpu

epsilon = 0.05
AXES = ("group", "blk")


def exchange(x, bits, count):
    route = [(i, i ^ (1 << bits[i & 1])) for i in range(count)]
    return lax.ppermute(x, AXES, route)


def place(x, order):
    return sum(((x >> bit) & 1) << step for step, bit in enumerate(order))


def tail(features, factor, src_ref, early_ref, last_ref, logits_ref, stats_ref, terms_ref,
         col_ref, pot_ref):
    block = last_ref[...]
    rows = block[:, :features]
    pots = block[:, features:features + 1].astype(jnp.float32)
    offset = pots / epsilon - jnp.sum(jnp.square(rows.astype(jnp.float32)), 1, keepdims=True) / (
        features * epsilon
    )
    late = lax.dot_general(
        rows, src_ref[...], (((1,), (1,)), ((), ())), preferred_element_type=jnp.float32
    ) * factor + offset
    late_max = jnp.max(late, 0, keepdims=True)
    late_sum = jnp.sum(jnp.exp(late - late_max), 0, keepdims=True)
    early_max = stats_ref[0:1, :]
    row_max = jnp.maximum(early_max, late_max)
    row_lse = row_max + jnp.log(
        stats_ref[1:2, :] * jnp.exp(early_max - row_max) + late_sum * jnp.exp(late_max - row_max)
    )
    dual = terms_ref[1:2, :] - row_lse
    pot_ref[...] = epsilon * dual + terms_ref[0:1, :]
    half = block.shape[0]
    for start, logits, block_pots in (
        (0, logits_ref[...], early_ref[:, features:features + 1].astype(jnp.float32)),
        (half, late, pots),
    ):
        column = logits - block_pots / epsilon + dual
        col_max = jnp.max(column, 1, keepdims=True)
        col_ref[start:start + half, 0:1] = col_max
        col_ref[start:start + half, 1:2] = jnp.sum(jnp.exp(column - col_max), 1, keepdims=True)

def per_device(sources, targets, target_potential, log_source_mass, log_target_mass):
    count = lax.axis_size("group") * lax.axis_size("blk")
    levels = count.bit_length() - 1
    if (1 << levels) != count:
        raise ValueError("count not pow2")
    outer = list(range(levels - 1, 0, -1))
    swapped = []
    for j in range(0, len(outer) - 1, 2):
        swapped += [outer[j + 1], outer[j]]
    swapped += outer[len(swapped):]
    orders = (outer, swapped)
    features = sources.shape[1]
    factor = 2.0 / (features * epsilon)

    lane = lax.broadcasted_iota(jnp.int32, (targets.shape[0], features + 128), 1)
    held = lax.optimization_barrier(
        jnp.where(
            lane < features,
            jnp.pad(targets, ((0, 0), (0, 128))),
            target_potential[:, None],
        )
    )
    source_terms = lax.optimization_barrier(
        jnp.stack(
            [
                jnp.sum(jnp.square(sources.astype(jnp.float32)), 1) / features,
                log_source_mass,
            ]
        )
    )
    for bits in zip(*orders):
        held = jnp.concatenate([held, exchange(held, bits, count)], 0)
    last = exchange(held, (0, 0), count)

    early_rows = held[:, :features]
    early_pots = held[:, features].astype(jnp.float32)
    early_offset = early_pots / epsilon - jnp.sum(
        jnp.square(early_rows.astype(jnp.float32)), 1
    ) / (features * epsilon)
    early_logits = lax.dot_general(
        early_rows, sources, (((1,), (1,)), ((), ())), preferred_element_type=jnp.float32
    ) * factor + early_offset[:, None]
    early_max = jnp.max(early_logits, 0)
    early_stats = jnp.stack([early_max, jnp.sum(jnp.exp(early_logits - early_max[None, :]), 0)])

    half = held.shape[0]
    vmem = pl.BlockSpec(memory_space=pltpu.VMEM)
    columns, source_potential = pl.pallas_call(
        functools.partial(tail, features, factor),
        out_shape=(
            jax.ShapeDtypeStruct((2 * half, 2), jnp.float32),
            jax.ShapeDtypeStruct((1, sources.shape[0]), jnp.float32),
        ),
        in_specs=[vmem] * 6,
        out_specs=(vmem, vmem),
        compiler_params=pltpu.CompilerParams(vmem_limit_bytes=24 * 1024 * 1024),
    )(sources, held, last, early_logits, early_stats, source_terms)
    source_potential = source_potential.reshape(-1)

    me = lax.axis_index(AXES)
    width = columns.shape[0] // count
    apart = me ^ (jnp.arange(count * width) // width)
    mine = jnp.where(me & 1 == 0, place(apart, orders[0]), place(apart, orders[1]))
    other = jnp.where(me & 1 == 0, place(apart, orders[1]), place(apart, orders[0]))
    where = jnp.where(apart & 1 == 0, mine, count // 2 + other)
    where = where * width + jnp.arange(count * width) % width
    choose = (where[:, None] == jnp.arange(count * width)[None, :]).astype(jnp.float32)
    part = jnp.dot(choose, columns, precision=lax.Precision.HIGHEST).reshape(count, width, 2)
    part = lax.all_to_all(part, AXES, 0, 0, tiled=True)
    owned_max = jnp.max(part[:, :, 0], 0)
    owned_sum = jnp.sum(part[:, :, 1] * jnp.exp(part[:, :, 0] - owned_max[None, :]), 0)
    part = (owned_max, owned_sum)

    target_update = epsilon * (log_target_mass - (part[0] + jnp.log(part[1])))
    return (source_potential, target_update)


def solution(mesh):
    return jax.shard_map(
        per_device,
        mesh=mesh,
        in_specs=(
            P(AXES, None),
            P(AXES, None),
            P(AXES),
            P(AXES),
            P(AXES),
        ),
        out_specs=(P(AXES), P(AXES)),
        check_vma=False,
    )
```

```python
import functools

import jax
import jax.numpy as jnp
from jax import lax
from jax.sharding import PartitionSpec as P
from jax.experimental import pallas as pl
from jax.experimental.pallas import tpu as pltpu

epsilon = 0.05
AXES = ("group", "blk")


def exchange(x, bit, count):
    route = [(i, i ^ (1 << bit)) for i in range(count)]
    return lax.ppermute(x, AXES, route)


def tail(features, factor, src_ref, early_ref, last_ref, logits_ref, stats_ref, terms_ref,
         col_ref, pot_ref):
    block = last_ref[...]
    rows = block[:, :features]
    pots = block[:, features:features + 1].astype(jnp.float32)
    offset = pots / epsilon - jnp.sum(jnp.square(rows.astype(jnp.float32)), 1, keepdims=True) / (
        features * epsilon
    )
    late = lax.dot_general(
        rows, src_ref[...], (((1,), (1,)), ((), ())), preferred_element_type=jnp.float32
    ) * factor + offset
    late_max = jnp.max(late, 0, keepdims=True)
    late_sum = jnp.sum(jnp.exp(late - late_max), 0, keepdims=True)
    early_max = stats_ref[0:1, :]
    row_max = jnp.maximum(early_max, late_max)
    row_lse = row_max + jnp.log(
        stats_ref[1:2, :] * jnp.exp(early_max - row_max) + late_sum * jnp.exp(late_max - row_max)
    )
    dual = terms_ref[1:2, :] - row_lse
    pot_ref[...] = epsilon * dual + terms_ref[0:1, :]
    half = block.shape[0]
    for start, logits, block_pots in (
        (0, logits_ref[...], early_ref[:, features:features + 1].astype(jnp.float32)),
        (half, late, pots),
    ):
        column = logits - block_pots / epsilon + dual
        col_max = jnp.max(column, 1, keepdims=True)
        col_ref[start:start + half, 0:1] = col_max
        col_ref[start:start + half, 1:2] = jnp.sum(jnp.exp(column - col_max), 1, keepdims=True)

def per_device(sources, targets, target_potential, log_source_mass, log_target_mass):
    count = lax.axis_size("group") * lax.axis_size("blk")
    levels = count.bit_length() - 1
    if (1 << levels) != count:
        raise ValueError("count not pow2")
    order = list(reversed(range(levels)))
    features = sources.shape[1]
    factor = 2.0 / (features * epsilon)

    def pack(rows, pots):
        lane = lax.broadcasted_iota(jnp.int32, (rows.shape[0], features + 128), 1)
        return jnp.where(lane < features, jnp.pad(rows, ((0, 0), (0, 128))), pots[:, None])

    got_rows = exchange(targets, order[0], count)
    got_pots = exchange(target_potential, order[0], count)
    held = lax.optimization_barrier(pack(targets, target_potential))
    held = jnp.concatenate([held, pack(got_rows, got_pots)], 0)
    source_terms = lax.optimization_barrier(
        jnp.stack(
            [
                jnp.sum(jnp.square(sources.astype(jnp.float32)), 1) / features,
                log_source_mass,
            ]
        )
    )
    for bit in order[1:-1]:
        held = jnp.concatenate([held, exchange(held, bit, count)], 0)
    last = exchange(held, order[-1], count)

    early_rows = held[:, :features]
    early_pots = held[:, features].astype(jnp.float32)
    early_offset = early_pots / epsilon - jnp.sum(
        jnp.square(early_rows.astype(jnp.float32)), 1
    ) / (features * epsilon)
    early_logits = lax.dot_general(
        early_rows, sources, (((1,), (1,)), ((), ())), preferred_element_type=jnp.float32
    ) * factor + early_offset[:, None]
    early_max = jnp.max(early_logits, 0)
    early_stats = jnp.stack([early_max, jnp.sum(jnp.exp(early_logits - early_max[None, :]), 0)])

    half = held.shape[0]
    vmem = pl.BlockSpec(memory_space=pltpu.VMEM)
    columns, source_potential = pl.pallas_call(
        functools.partial(tail, features, factor),
        out_shape=(
            jax.ShapeDtypeStruct((2 * half, 2), jnp.float32),
            jax.ShapeDtypeStruct((1, sources.shape[0]), jnp.float32),
        ),
        in_specs=[vmem] * 6,
        out_specs=(vmem, vmem),
        compiler_params=pltpu.CompilerParams(vmem_limit_bytes=24 * 1024 * 1024),
    )(sources, held, last, early_logits, early_stats, source_terms)
    source_potential = source_potential.reshape(-1)

    me = lax.axis_index(AXES)
    width = columns.shape[0] // count
    apart = me ^ (jnp.arange(count * width) // width)
    where = sum(((apart >> bit) & 1) << step for step, bit in enumerate(order))
    where = where * width + jnp.arange(count * width) % width
    choose = (where[:, None] == jnp.arange(count * width)[None, :]).astype(jnp.float32)
    part = jnp.dot(choose, columns, precision=lax.Precision.HIGHEST).reshape(count, width, 2)
    part = lax.all_to_all(part, AXES, 0, 0, tiled=True)
    owned_max = jnp.max(part[:, :, 0], 0)
    owned_sum = jnp.sum(part[:, :, 1] * jnp.exp(part[:, :, 0] - owned_max[None, :]), 0)
    part = (owned_max, owned_sum)

    target_update = epsilon * (log_target_mass - (part[0] + jnp.log(part[1])))
    return (source_potential, target_update)


def solution(mesh):
    return jax.shard_map(
        per_device,
        mesh=mesh,
        in_specs=(
            P(AXES, None),
            P(AXES, None),
            P(AXES),
            P(AXES),
            P(AXES),
        ),
        out_specs=(P(AXES), P(AXES)),
        check_vma=False,
    )
```

```python
import functools

import jax
import jax.numpy as jnp
from jax import lax
from jax.sharding import PartitionSpec as P
from jax.experimental import pallas as pl
from jax.experimental.pallas import tpu as pltpu

epsilon = 0.05
AXES = ("group", "blk")


def exchange(x, bit, count):
    route = [(i, i ^ (1 << bit)) for i in range(count)]
    return lax.ppermute(x, AXES, route)


def tail(features, factor, width, order, me_ref, src_ref, early_ref, last_ref, logits_ref,
         stats_ref, terms_ref, col_ref, pot_ref):
    block = last_ref[...]
    rows = block[:, :features]
    pots = block[:, features:features + 1].astype(jnp.float32)
    offset = pots / epsilon - jnp.sum(jnp.square(rows.astype(jnp.float32)), 1, keepdims=True) / (
        features * epsilon
    )
    late = lax.dot_general(
        rows, src_ref[...], (((1,), (1,)), ((), ())), preferred_element_type=jnp.float32
    ) * factor + offset
    late_max = jnp.max(late, 0, keepdims=True)
    late_sum = jnp.sum(jnp.exp(late - late_max), 0, keepdims=True)
    early_max = stats_ref[0:1, :]
    row_max = jnp.maximum(early_max, late_max)
    row_lse = row_max + jnp.log(
        stats_ref[1:2, :] * jnp.exp(early_max - row_max) + late_sum * jnp.exp(late_max - row_max)
    )
    dual = terms_ref[1:2, :] - row_lse
    pot_ref[...] = epsilon * dual + terms_ref[0:1, :]
    half = block.shape[0]
    for start, logits, block_pots in (
        (0, logits_ref[...], early_ref[:, features:features + 1].astype(jnp.float32)),
        (half, late, pots),
    ):
        column = logits - block_pots / epsilon + dual
        col_max = jnp.max(column, 1, keepdims=True)
        col_sum = jnp.sum(jnp.exp(column - col_max), 1, keepdims=True)
        for first in range(0, half, width):
            position = (start + first) // width
            owner = me_ref[0] ^ sum(((position >> step) & 1) << bit for step, bit in enumerate(order))
            slot = pl.ds(pl.multiple_of(owner * width, width), width)
            col_ref[slot, 0:1] = col_max[first:first + width]
            col_ref[slot, 1:2] = col_sum[first:first + width]

def per_device(sources, targets, target_potential, log_source_mass, log_target_mass):
    count = lax.axis_size("group") * lax.axis_size("blk")
    levels = count.bit_length() - 1
    if (1 << levels) != count:
        raise ValueError("count not pow2")
    order = list(reversed(range(levels)))
    features = sources.shape[1]
    factor = 2.0 / (features * epsilon)

    lane = lax.broadcasted_iota(jnp.int32, (targets.shape[0], features + 128), 1)
    held = lax.optimization_barrier(
        jnp.where(
            lane < features,
            jnp.pad(targets, ((0, 0), (0, 128))),
            target_potential[:, None],
        )
    )
    source_terms = lax.optimization_barrier(
        jnp.stack(
            [
                jnp.sum(jnp.square(sources.astype(jnp.float32)), 1) / features,
                log_source_mass,
            ]
        )
    )
    for bit in order[:-1]:
        held = jnp.concatenate([held, exchange(held, bit, count)], 0)
    last = exchange(held, order[-1], count)

    early_rows = held[:, :features]
    early_pots = held[:, features].astype(jnp.float32)
    early_offset = early_pots / epsilon - jnp.sum(
        jnp.square(early_rows.astype(jnp.float32)), 1
    ) / (features * epsilon)
    early_logits = lax.dot_general(
        early_rows, sources, (((1,), (1,)), ((), ())), preferred_element_type=jnp.float32
    ) * factor + early_offset[:, None]
    early_max = jnp.max(early_logits, 0)
    early_stats = jnp.stack([early_max, jnp.sum(jnp.exp(early_logits - early_max[None, :]), 0)])

    half = held.shape[0]
    width = targets.shape[0]
    me = lax.axis_index(AXES)
    vmem = pl.BlockSpec(memory_space=pltpu.VMEM)
    columns, source_potential = pl.pallas_call(
        functools.partial(tail, features, factor, width, order),
        out_shape=(
            jax.ShapeDtypeStruct((2 * half, 2), jnp.float32),
            jax.ShapeDtypeStruct((1, sources.shape[0]), jnp.float32),
        ),
        in_specs=[pl.BlockSpec(memory_space=pltpu.SMEM)] + [vmem] * 6,
        out_specs=(vmem, vmem),
        compiler_params=pltpu.CompilerParams(vmem_limit_bytes=24 * 1024 * 1024),
    )(me.astype(jnp.int32).reshape(1), sources, held, last, early_logits, early_stats, source_terms)
    source_potential = source_potential.reshape(-1)

    part = columns.reshape(count, width, 2)
    part = lax.all_to_all(part, AXES, 0, 0, tiled=True)
    owned_max = jnp.max(part[:, :, 0], 0)
    owned_sum = jnp.sum(part[:, :, 1] * jnp.exp(part[:, :, 0] - owned_max[None, :]), 0)
    part = (owned_max, owned_sum)

    target_update = epsilon * (log_target_mass - (part[0] + jnp.log(part[1])))
    return (source_potential, target_update)


def solution(mesh):
    return jax.shard_map(
        per_device,
        mesh=mesh,
        in_specs=(
            P(AXES, None),
            P(AXES, None),
            P(AXES),
            P(AXES),
            P(AXES),
        ),
        out_specs=(P(AXES), P(AXES)),
        check_vma=False,
    )
```

```python
import functools

import jax
import jax.numpy as jnp
from jax import lax
from jax.sharding import PartitionSpec as P
from jax.experimental import pallas as pl
from jax.experimental.pallas import tpu as pltpu

epsilon = 0.05
AXES = ("group", "blk")


def exchange(x, bit, count):
    route = [(i, i ^ (1 << bit)) for i in range(count)]
    return lax.ppermute(x, AXES, route)


def tail(features, factor, width, order, me_ref, src_ref, early_ref, last_ref, logits_ref,
         stats_ref, terms_ref, col_ref, pot_ref):
    block = last_ref[...]
    rows = block[:, :features]
    pots = block[:, features:features + 1].astype(jnp.float32)
    offset = pots / epsilon - jnp.sum(jnp.square(rows.astype(jnp.float32)), 1, keepdims=True) / (
        features * epsilon
    )
    late = lax.dot_general(
        rows, src_ref[...], (((1,), (1,)), ((), ())), preferred_element_type=jnp.float32
    ) * factor + offset
    late_max = jnp.max(late, 0, keepdims=True)
    late_sum = jnp.sum(jnp.exp(late - late_max), 0, keepdims=True)
    early_max = stats_ref[0:1, :]
    row_max = jnp.maximum(early_max, late_max)
    row_lse = row_max + jnp.log(
        stats_ref[1:2, :] * jnp.exp(early_max - row_max) + late_sum * jnp.exp(late_max - row_max)
    )
    dual = terms_ref[1:2, :] - row_lse
    pot_ref[...] = epsilon * dual + terms_ref[0:1, :]
    half = block.shape[0]
    for start, logits, block_pots in (
        (0, logits_ref[...], early_ref[:, features:features + 1].astype(jnp.float32)),
        (half, late, pots),
    ):
        column = logits - block_pots / epsilon + dual
        col_max = jnp.max(column, 1, keepdims=True)
        col_sum = jnp.sum(jnp.exp(column - col_max), 1, keepdims=True)
        diagonal = lax.broadcasted_iota(jnp.int32, (width, width), 0) == lax.broadcasted_iota(
            jnp.int32, (width, width), 1
        )
        for first in range(0, half, width):
            position = (start + first) // width
            owner = me_ref[0] ^ sum(((position >> step) & 1) << bit for step, bit in enumerate(order))
            for lanes, stat in ((0, col_max), (width, col_sum)):
                piece = jnp.where(diagonal, stat[first:first + width], 0.0)
                col_ref[pl.ds(owner, 1), lanes:lanes + width] = jnp.sum(piece, 0, keepdims=True)

def per_device(sources, targets, target_potential, log_source_mass, log_target_mass):
    count = lax.axis_size("group") * lax.axis_size("blk")
    levels = count.bit_length() - 1
    if (1 << levels) != count:
        raise ValueError("count not pow2")
    order = list(reversed(range(levels)))
    features = sources.shape[1]
    factor = 2.0 / (features * epsilon)

    lane = lax.broadcasted_iota(jnp.int32, (targets.shape[0], features + 128), 1)
    held = lax.optimization_barrier(
        jnp.where(
            lane < features,
            jnp.pad(targets, ((0, 0), (0, 128))),
            target_potential[:, None],
        )
    )
    source_terms = lax.optimization_barrier(
        jnp.stack(
            [
                jnp.sum(jnp.square(sources.astype(jnp.float32)), 1) / features,
                log_source_mass,
            ]
        )
    )
    for bit in order[:-1]:
        held = jnp.concatenate([held, exchange(held, bit, count)], 0)
    last = exchange(held, order[-1], count)

    early_rows = held[:, :features]
    early_pots = held[:, features].astype(jnp.float32)
    early_offset = early_pots / epsilon - jnp.sum(
        jnp.square(early_rows.astype(jnp.float32)), 1
    ) / (features * epsilon)
    early_logits = lax.dot_general(
        early_rows, sources, (((1,), (1,)), ((), ())), preferred_element_type=jnp.float32
    ) * factor + early_offset[:, None]
    early_max = jnp.max(early_logits, 0)
    early_stats = jnp.stack([early_max, jnp.sum(jnp.exp(early_logits - early_max[None, :]), 0)])

    half = held.shape[0]
    width = targets.shape[0]
    me = lax.axis_index(AXES)
    vmem = pl.BlockSpec(memory_space=pltpu.VMEM)
    columns, source_potential = pl.pallas_call(
        functools.partial(tail, features, factor, width, order),
        out_shape=(
            jax.ShapeDtypeStruct((count, 2 * width), jnp.float32),
            jax.ShapeDtypeStruct((1, sources.shape[0]), jnp.float32),
        ),
        in_specs=[pl.BlockSpec(memory_space=pltpu.SMEM)] + [vmem] * 6,
        out_specs=(vmem, vmem),
        compiler_params=pltpu.CompilerParams(vmem_limit_bytes=24 * 1024 * 1024),
    )(me.astype(jnp.int32).reshape(1), sources, held, last, early_logits, early_stats, source_terms)
    source_potential = source_potential.reshape(-1)

    part = lax.all_to_all(columns, AXES, 0, 0, tiled=True)
    owned_max = jnp.max(part[:, :width], 0)
    owned_sum = jnp.sum(part[:, width:] * jnp.exp(part[:, :width] - owned_max[None, :]), 0)
    part = (owned_max, owned_sum)

    target_update = epsilon * (log_target_mass - (part[0] + jnp.log(part[1])))
    return (source_potential, target_update)


def solution(mesh):
    return jax.shard_map(
        per_device,
        mesh=mesh,
        in_specs=(
            P(AXES, None),
            P(AXES, None),
            P(AXES),
            P(AXES),
            P(AXES),
        ),
        out_specs=(P(AXES), P(AXES)),
        check_vma=False,
    )
```

```python
import functools

import jax
import jax.numpy as jnp
from jax import lax
from jax.sharding import PartitionSpec as P
from jax.experimental import pallas as pl
from jax.experimental.pallas import tpu as pltpu

epsilon = 0.05
AXES = ("group", "blk")


def exchange(x, bit, count):
    route = [(i, i ^ (1 << bit)) for i in range(count)]
    return lax.ppermute(x, AXES, route)


def tail(features, factor, width, order, me_ref, src_ref, early_ref, last_ref, logits_ref,
         stats_ref, terms_ref, col_ref, pot_ref):
    block = last_ref[...]
    rows = block[:, :features]
    pots = block[:, features:features + 1].astype(jnp.float32)
    offset = pots / epsilon - jnp.sum(jnp.square(rows.astype(jnp.float32)), 1, keepdims=True) / (
        features * epsilon
    )
    late = lax.dot_general(
        rows, src_ref[...], (((1,), (1,)), ((), ())), preferred_element_type=jnp.float32
    ) * factor + offset
    late_max = jnp.max(late, 0, keepdims=True)
    late_sum = jnp.sum(jnp.exp(late - late_max), 0, keepdims=True)
    early_max = stats_ref[0:1, :]
    row_max = jnp.maximum(early_max, late_max)
    row_lse = row_max + jnp.log(
        stats_ref[1:2, :] * jnp.exp(early_max - row_max) + late_sum * jnp.exp(late_max - row_max)
    )
    dual = terms_ref[1:2, :] - row_lse
    pot_ref[...] = epsilon * dual + terms_ref[0:1, :]
    half = block.shape[0]
    for start, logits, block_pots in (
        (0, logits_ref[...], early_ref[:, features:features + 1].astype(jnp.float32)),
        (half, late, pots),
    ):
        column = logits - block_pots / epsilon + dual
        col_max = jnp.max(column, 1, keepdims=True)
        col_sum = jnp.sum(jnp.exp(column - col_max), 1, keepdims=True)
        diagonal = lax.broadcasted_iota(jnp.int32, (width, width), 0) == lax.broadcasted_iota(
            jnp.int32, (width, width), 1
        )
        for first in range(0, half, width):
            position = (start + first) // width
            owner = me_ref[0] ^ sum(((position >> step) & 1) << bit for step, bit in enumerate(order))
            for lanes, stat in ((0, col_max), (width, col_sum)):
                piece = jnp.where(diagonal, stat[first:first + width], 0.0)
                col_ref[pl.ds(owner, 1), lanes:lanes + width] = jnp.sum(piece, 0, keepdims=True)

def per_device(sources, targets, target_potential, log_source_mass, log_target_mass):
    count = lax.axis_size("group") * lax.axis_size("blk")
    levels = count.bit_length() - 1
    if (1 << levels) != count:
        raise ValueError("count not pow2")
    order = list(reversed(range(levels)))
    order[0], order[1] = order[1], order[0]
    features = sources.shape[1]
    factor = 2.0 / (features * epsilon)

    lane = lax.broadcasted_iota(jnp.int32, (targets.shape[0], features + 128), 1)
    held = lax.optimization_barrier(
        jnp.where(
            lane < features,
            jnp.pad(targets, ((0, 0), (0, 128))),
            target_potential[:, None],
        )
    )
    source_terms = lax.optimization_barrier(
        jnp.stack(
            [
                jnp.sum(jnp.square(sources.astype(jnp.float32)), 1) / features,
                log_source_mass,
            ]
        )
    )
    for bit in order[:-1]:
        held = jnp.concatenate([held, exchange(held, bit, count)], 0)
    last = exchange(held, order[-1], count)

    early_rows = held[:, :features]
    early_pots = held[:, features].astype(jnp.float32)
    early_offset = early_pots / epsilon - jnp.sum(
        jnp.square(early_rows.astype(jnp.float32)), 1
    ) / (features * epsilon)
    early_logits = lax.dot_general(
        early_rows, sources, (((1,), (1,)), ((), ())), preferred_element_type=jnp.float32
    ) * factor + early_offset[:, None]
    early_max = jnp.max(early_logits, 0)
    early_stats = jnp.stack([early_max, jnp.sum(jnp.exp(early_logits - early_max[None, :]), 0)])

    half = held.shape[0]
    width = targets.shape[0]
    me = lax.axis_index(AXES)
    vmem = pl.BlockSpec(memory_space=pltpu.VMEM)
    columns, source_potential = pl.pallas_call(
        functools.partial(tail, features, factor, width, order),
        out_shape=(
            jax.ShapeDtypeStruct((count, 2 * width), jnp.float32),
            jax.ShapeDtypeStruct((1, sources.shape[0]), jnp.float32),
        ),
        in_specs=[pl.BlockSpec(memory_space=pltpu.SMEM)] + [vmem] * 6,
        out_specs=(vmem, vmem),
        compiler_params=pltpu.CompilerParams(vmem_limit_bytes=24 * 1024 * 1024),
    )(me.astype(jnp.int32).reshape(1), sources, held, last, early_logits, early_stats, source_terms)
    source_potential = source_potential.reshape(-1)

    part = lax.all_to_all(columns, AXES, 0, 0, tiled=True)
    owned_max = jnp.max(part[:, :width], 0)
    owned_sum = jnp.sum(part[:, width:] * jnp.exp(part[:, :width] - owned_max[None, :]), 0)
    part = (owned_max, owned_sum)

    target_update = epsilon * (log_target_mass - (part[0] + jnp.log(part[1])))
    return (source_potential, target_update)


def solution(mesh):
    return jax.shard_map(
        per_device,
        mesh=mesh,
        in_specs=(
            P(AXES, None),
            P(AXES, None),
            P(AXES),
            P(AXES),
            P(AXES),
        ),
        out_specs=(P(AXES), P(AXES)),
        check_vma=False,
    )
```

```python
import functools

import jax
import jax.numpy as jnp
from jax import lax
from jax.sharding import PartitionSpec as P
from jax.experimental import pallas as pl
from jax.experimental.pallas import tpu as pltpu

epsilon = 0.05
AXES = ("group", "blk")


def exchange(x, bit, count):
    route = [(i, i ^ (1 << bit)) for i in range(count)]
    return lax.ppermute(x, AXES, route)


def tail(features, factor, width, src_ref, rows_ref, terms_ref, col_ref, pot_ref):
    block = rows_ref[...]
    rows = block[:, :features]
    pots = block[:, features:features + 1].astype(jnp.float32)
    offset = pots / epsilon - jnp.sum(jnp.square(rows.astype(jnp.float32)), 1, keepdims=True) / (
        features * epsilon
    )
    logits = lax.dot_general(
        rows, src_ref[...], (((1,), (1,)), ((), ())), preferred_element_type=jnp.float32
    ) * factor + offset
    row_max = jnp.max(logits, 0, keepdims=True)
    row_lse = row_max + jnp.log(jnp.sum(jnp.exp(logits - row_max), 0, keepdims=True))
    dual = terms_ref[1:2, :] - row_lse
    pot_ref[...] = epsilon * dual + terms_ref[0:1, :]
    column = logits - pots / epsilon + dual
    col_max = jnp.max(column, 1, keepdims=True)
    col_sum = jnp.sum(jnp.exp(column - col_max), 1, keepdims=True)
    diagonal = lax.broadcasted_iota(jnp.int32, (width, width), 0) == lax.broadcasted_iota(
        jnp.int32, (width, width), 1
    )
    for owner in range(block.shape[0] // width):
        first = owner * width
        for lanes, stat in ((0, col_max), (width, col_sum)):
            piece = jnp.where(diagonal, stat[first:first + width], 0.0)
            col_ref[owner:owner + 1, lanes:lanes + width] = jnp.sum(piece, 0, keepdims=True)


def per_device(sources, targets, target_potential, log_source_mass, log_target_mass):
    count = lax.axis_size("group") * lax.axis_size("blk")
    levels = count.bit_length() - 1
    if (1 << levels) != count:
        raise ValueError("count not pow2")
    order = list(reversed(range(levels)))
    features = sources.shape[1]
    factor = 2.0 / (features * epsilon)

    lane = lax.broadcasted_iota(jnp.int32, (targets.shape[0], features + 128), 1)
    held = lax.optimization_barrier(
        jnp.where(
            lane < features,
            jnp.pad(targets, ((0, 0), (0, 128))),
            target_potential[:, None],
        )
    )
    source_terms = lax.optimization_barrier(
        jnp.stack(
            [
                jnp.sum(jnp.square(sources.astype(jnp.float32)), 1) / features,
                log_source_mass,
            ]
        )
    )
    everything = lax.all_to_all(
        jnp.broadcast_to(held[None], (count,) + held.shape), AXES, 0, 0, tiled=True
    ).reshape(count * held.shape[0], held.shape[1])

    width = targets.shape[0]
    vmem = pl.BlockSpec(memory_space=pltpu.VMEM)
    columns, source_potential = pl.pallas_call(
        functools.partial(tail, features, factor, width),
        out_shape=(
            jax.ShapeDtypeStruct((count, 2 * width), jnp.float32),
            jax.ShapeDtypeStruct((1, sources.shape[0]), jnp.float32),
        ),
        in_specs=[vmem] * 3,
        out_specs=(vmem, vmem),
        compiler_params=pltpu.CompilerParams(vmem_limit_bytes=24 * 1024 * 1024),
    )(sources, everything, source_terms)
    source_potential = source_potential.reshape(-1)

    part = lax.all_to_all(columns, AXES, 0, 0, tiled=True)
    owned_max = jnp.max(part[:, :width], 0)
    owned_sum = jnp.sum(part[:, width:] * jnp.exp(part[:, :width] - owned_max[None, :]), 0)
    part = (owned_max, owned_sum)

    target_update = epsilon * (log_target_mass - (part[0] + jnp.log(part[1])))
    return (source_potential, target_update)


def solution(mesh):
    return jax.shard_map(
        per_device,
        mesh=mesh,
        in_specs=(
            P(AXES, None),
            P(AXES, None),
            P(AXES),
            P(AXES),
            P(AXES),
        ),
        out_specs=(P(AXES), P(AXES)),
        check_vma=False,
    )
```

```python
import functools

import jax
import jax.numpy as jnp
from jax import lax
from jax.sharding import PartitionSpec as P
from jax.experimental import pallas as pl
from jax.experimental.pallas import tpu as pltpu

epsilon = 0.05
AXES = ("group", "blk")


def exchange(x, bit, count):
    route = [(i, i ^ (1 << bit)) for i in range(count)]
    return lax.ppermute(x, AXES, route)


def tail(features, factor, width, src_ref, rows_ref, terms_ref, col_ref, pot_ref):
    block = rows_ref[...]
    rows = block[:, :features]
    pots = block[:, features:features + 1].astype(jnp.float32)
    offset = pots / epsilon - jnp.sum(jnp.square(rows.astype(jnp.float32)), 1, keepdims=True) / (
        features * epsilon
    )
    logits = lax.dot_general(
        rows, src_ref[...], (((1,), (1,)), ((), ())), preferred_element_type=jnp.float32
    ) * factor + offset
    row_max = jnp.max(logits, 0, keepdims=True)
    row_lse = row_max + jnp.log(jnp.sum(jnp.exp(logits - row_max), 0, keepdims=True))
    dual = terms_ref[1:2, :] - row_lse
    pot_ref[...] = epsilon * dual + terms_ref[0:1, :]
    column = logits - pots / epsilon + dual
    col_max = jnp.max(column, 1, keepdims=True)
    col_sum = jnp.sum(jnp.exp(column - col_max), 1, keepdims=True)
    diagonal = lax.broadcasted_iota(jnp.int32, (width, width), 0) == lax.broadcasted_iota(
        jnp.int32, (width, width), 1
    )
    for owner in range(block.shape[0] // width):
        first = owner * width
        for lanes, stat in ((0, col_max), (width, col_sum)):
            piece = jnp.where(diagonal, stat[first:first + width], 0.0)
            col_ref[owner:owner + 1, lanes:lanes + width] = jnp.sum(piece, 0, keepdims=True)


def per_device(sources, targets, target_potential, log_source_mass, log_target_mass):
    count = lax.axis_size("group") * lax.axis_size("blk")
    levels = count.bit_length() - 1
    if (1 << levels) != count:
        raise ValueError("count not pow2")
    order = list(reversed(range(levels)))
    features = sources.shape[1]
    factor = 2.0 / (features * epsilon)

    lane = lax.broadcasted_iota(jnp.int32, (count, targets.shape[0], features + 128), 2)
    outgoing = jnp.where(
        lane < features,
        jnp.pad(targets, ((0, 0), (0, 128)))[None],
        target_potential[None, :, None],
    )
    source_terms = lax.optimization_barrier(
        jnp.stack(
            [
                jnp.sum(jnp.square(sources.astype(jnp.float32)), 1) / features,
                log_source_mass,
            ]
        )
    )
    everything = lax.all_to_all(outgoing, AXES, 0, 0, tiled=True).reshape(
        count * targets.shape[0], features + 128
    )

    width = targets.shape[0]
    vmem = pl.BlockSpec(memory_space=pltpu.VMEM)
    columns, source_potential = pl.pallas_call(
        functools.partial(tail, features, factor, width),
        out_shape=(
            jax.ShapeDtypeStruct((count, 2 * width), jnp.float32),
            jax.ShapeDtypeStruct((1, sources.shape[0]), jnp.float32),
        ),
        in_specs=[vmem] * 3,
        out_specs=(vmem, vmem),
        compiler_params=pltpu.CompilerParams(vmem_limit_bytes=24 * 1024 * 1024),
    )(sources, everything, source_terms)
    source_potential = source_potential.reshape(-1)

    part = lax.all_to_all(columns, AXES, 0, 0, tiled=True)
    owned_max = jnp.max(part[:, :width], 0)
    owned_sum = jnp.sum(part[:, width:] * jnp.exp(part[:, :width] - owned_max[None, :]), 0)
    part = (owned_max, owned_sum)

    target_update = epsilon * (log_target_mass - (part[0] + jnp.log(part[1])))
    return (source_potential, target_update)


def solution(mesh):
    return jax.shard_map(
        per_device,
        mesh=mesh,
        in_specs=(
            P(AXES, None),
            P(AXES, None),
            P(AXES),
            P(AXES),
            P(AXES),
        ),
        out_specs=(P(AXES), P(AXES)),
        check_vma=False,
    )
```

```python
import functools

import jax
import jax.numpy as jnp
from jax import lax
from jax.sharding import PartitionSpec as P
from jax.experimental import pallas as pl
from jax.experimental.pallas import tpu as pltpu

epsilon = 0.05
AXES = ("group", "blk")


def exchange(x, bit, count):
    route = [(i, i ^ (1 << bit)) for i in range(count)]
    return lax.ppermute(x, AXES, route)


def tail(features, factor, width, src_ref, rows_ref, terms_ref, col_ref, dual_ref):
    block = rows_ref[...]
    rows = block[:, :features]
    pots = block[:, features:features + 1].astype(jnp.float32)
    offset = pots / epsilon - jnp.sum(jnp.square(rows.astype(jnp.float32)), 1, keepdims=True) / (
        features * epsilon
    )
    logits = lax.dot_general(
        rows, src_ref[...], (((1,), (1,)), ((), ())), preferred_element_type=jnp.float32
    ) * factor + offset
    row_max = jnp.max(logits, 0, keepdims=True)
    row_lse = row_max + jnp.log(jnp.sum(jnp.exp(logits - row_max), 0, keepdims=True))
    dual = terms_ref[1:2, :] - row_lse
    dual_ref[...] = dual
    column = logits - pots / epsilon + dual
    col_max = jnp.max(column, 1, keepdims=True)
    col_sum = jnp.sum(jnp.exp(column - col_max), 1, keepdims=True)
    diagonal = lax.broadcasted_iota(jnp.int32, (width, width), 0) == lax.broadcasted_iota(
        jnp.int32, (width, width), 1
    )
    for owner in range(block.shape[0] // width):
        first = owner * width
        for lanes, stat in ((0, col_max), (width, col_sum)):
            piece = jnp.where(diagonal, stat[first:first + width], 0.0)
            col_ref[owner:owner + 1, lanes:lanes + width] = jnp.sum(piece, 0, keepdims=True)


def per_device(sources, targets, target_potential, log_source_mass, log_target_mass):
    count = lax.axis_size("group") * lax.axis_size("blk")
    levels = count.bit_length() - 1
    if (1 << levels) != count:
        raise ValueError("count not pow2")
    order = list(reversed(range(levels)))
    features = sources.shape[1]
    factor = 2.0 / (features * epsilon)

    lane = lax.broadcasted_iota(jnp.int32, (targets.shape[0], features + 128), 1)
    held = lax.optimization_barrier(
        jnp.where(
            lane < features,
            jnp.pad(targets, ((0, 0), (0, 128))),
            target_potential[:, None],
        )
    )
    source_terms = lax.optimization_barrier(
        jnp.stack(
            [
                jnp.sum(jnp.square(sources.astype(jnp.float32)), 1) / features,
                log_source_mass,
            ]
        )
    )
    everything = lax.all_to_all(
        jnp.broadcast_to(held[None], (count,) + held.shape), AXES, 0, 0, tiled=True
    ).reshape(count * held.shape[0], held.shape[1])

    width = targets.shape[0]
    vmem = pl.BlockSpec(memory_space=pltpu.VMEM)
    columns, source_dual = pl.pallas_call(
        functools.partial(tail, features, factor, width),
        out_shape=(
            jax.ShapeDtypeStruct((count, 2 * width), jnp.float32),
            jax.ShapeDtypeStruct((1, sources.shape[0]), jnp.float32),
        ),
        in_specs=[vmem] * 3,
        out_specs=(vmem, vmem),
        compiler_params=pltpu.CompilerParams(vmem_limit_bytes=24 * 1024 * 1024),
    )(sources, everything, source_terms)
    source_potential = epsilon * source_dual.reshape(-1) + source_terms[0]

    part = lax.all_to_all(columns, AXES, 0, 0, tiled=True)
    owned_max = jnp.max(part[:, :width], 0)
    owned_sum = jnp.sum(part[:, width:] * jnp.exp(part[:, :width] - owned_max[None, :]), 0)
    part = (owned_max, owned_sum)

    target_update = epsilon * (log_target_mass - (part[0] + jnp.log(part[1])))
    return (source_potential, target_update)


def solution(mesh):
    return jax.shard_map(
        per_device,
        mesh=mesh,
        in_specs=(
            P(AXES, None),
            P(AXES, None),
            P(AXES),
            P(AXES),
            P(AXES),
        ),
        out_specs=(P(AXES), P(AXES)),
        check_vma=False,
    )
```

```python
import functools

import jax
import jax.numpy as jnp
from jax import lax
from jax.sharding import PartitionSpec as P
from jax.experimental import pallas as pl
from jax.experimental.pallas import tpu as pltpu

epsilon = 0.05
AXES = ("group", "blk")


def tail(features, factor, width, src_ref, rows_ref, terms_ref, col_ref, pot_ref):
    block = rows_ref[...]
    rows = block[:, :features]
    pots = block[:, features:features + 1].astype(jnp.float32)
    offset = pots / epsilon - jnp.sum(jnp.square(rows.astype(jnp.float32)), 1, keepdims=True) / (
        features * epsilon
    )
    logits = lax.dot_general(
        rows, src_ref[...], (((1,), (1,)), ((), ())), preferred_element_type=jnp.float32
    ) * factor + offset
    row_max = jnp.max(logits, 0, keepdims=True)
    row_lse = row_max + jnp.log(jnp.sum(jnp.exp(logits - row_max), 0, keepdims=True))
    dual = terms_ref[1:2, :] - row_lse
    pot_ref[...] = epsilon * dual + terms_ref[0:1, :]
    column = logits - pots / epsilon + dual
    col_max = jnp.max(column, 1, keepdims=True)
    col_sum = jnp.sum(jnp.exp(column - col_max), 1, keepdims=True)
    diagonal = lax.broadcasted_iota(jnp.int32, (width, width), 0) == lax.broadcasted_iota(
        jnp.int32, (width, width), 1
    )
    for owner in range(block.shape[0] // width):
        first = owner * width
        for lanes, stat in ((0, col_max), (width, col_sum)):
            piece = jnp.where(diagonal, stat[first:first + width], 0.0)
            col_ref[owner:owner + 1, lanes:lanes + width] = jnp.sum(piece, 0, keepdims=True)


def per_device(sources, targets, target_potential, log_source_mass, log_target_mass):
    count = lax.axis_size("group") * lax.axis_size("blk")
    features = sources.shape[1]
    factor = 2.0 / (features * epsilon)

    lane = lax.broadcasted_iota(jnp.int32, (targets.shape[0], features + 128), 1)
    held = lax.optimization_barrier(
        jnp.where(
            lane < features,
            jnp.pad(targets, ((0, 0), (0, 128))),
            target_potential[:, None],
        )
    )
    source_terms = lax.optimization_barrier(
        jnp.stack(
            [
                jnp.sum(jnp.square(sources.astype(jnp.float32)), 1) / features,
                log_source_mass,
            ]
        )
    )
    everything = lax.all_to_all(
        jnp.broadcast_to(held[None], (count,) + held.shape), AXES, 0, 0, tiled=True
    ).reshape(count * held.shape[0], held.shape[1])

    width = targets.shape[0]
    vmem = pl.BlockSpec(memory_space=pltpu.VMEM)
    columns, source_potential = pl.pallas_call(
        functools.partial(tail, features, factor, width),
        out_shape=(
            jax.ShapeDtypeStruct((count, 2 * width), jnp.float32),
            jax.ShapeDtypeStruct((1, sources.shape[0]), jnp.float32),
        ),
        in_specs=[vmem] * 3,
        out_specs=(vmem, vmem),
        compiler_params=pltpu.CompilerParams(vmem_limit_bytes=24 * 1024 * 1024),
    )(sources, everything, source_terms)
    source_potential = source_potential.reshape(-1)

    part = lax.all_to_all(columns, AXES, 0, 0, tiled=True)
    owned_max = jnp.max(part[:, :width], 0)
    owned_sum = jnp.sum(part[:, width:] * jnp.exp(part[:, :width] - owned_max[None, :]), 0)
    part = (owned_max, owned_sum)

    target_update = epsilon * (log_target_mass - (part[0] + jnp.log(part[1])))
    return (source_potential, target_update)


def solution(mesh):
    return jax.shard_map(
        per_device,
        mesh=mesh,
        in_specs=(
            P(AXES, None),
            P(AXES, None),
            P(AXES),
            P(AXES),
            P(AXES),
        ),
        out_specs=(P(AXES), P(AXES)),
        check_vma=False,
    )
```

```python
import functools

import jax
import jax.numpy as jnp
from jax import lax
from jax.sharding import PartitionSpec as P
from jax.experimental import pallas as pl
from jax.experimental.pallas import tpu as pltpu

epsilon = 0.05
AXES = ("group", "blk")


def tail(features, factor, width, src_ref, rows_ref, pots_ref, terms_ref, col_ref, pot_ref):
    block = rows = rows_ref[...]
    pots = pots_ref[:, 0:1].astype(jnp.float32)
    offset = pots / epsilon - jnp.sum(jnp.square(rows.astype(jnp.float32)), 1, keepdims=True) / (
        features * epsilon
    )
    logits = lax.dot_general(
        rows, src_ref[...], (((1,), (1,)), ((), ())), preferred_element_type=jnp.float32
    ) * factor + offset
    row_max = jnp.max(logits, 0, keepdims=True)
    row_lse = row_max + jnp.log(jnp.sum(jnp.exp(logits - row_max), 0, keepdims=True))
    dual = terms_ref[1:2, :] - row_lse
    pot_ref[...] = epsilon * dual + terms_ref[0:1, :]
    column = logits - pots / epsilon + dual
    col_max = jnp.max(column, 1, keepdims=True)
    col_sum = jnp.sum(jnp.exp(column - col_max), 1, keepdims=True)
    diagonal = lax.broadcasted_iota(jnp.int32, (width, width), 0) == lax.broadcasted_iota(
        jnp.int32, (width, width), 1
    )
    for owner in range(block.shape[0] // width):
        first = owner * width
        for lanes, stat in ((0, col_max), (width, col_sum)):
            piece = jnp.where(diagonal, stat[first:first + width], 0.0)
            col_ref[owner:owner + 1, lanes:lanes + width] = jnp.sum(piece, 0, keepdims=True)


def per_device(sources, targets, target_potential, log_source_mass, log_target_mass):
    count = lax.axis_size("group") * lax.axis_size("blk")
    features = sources.shape[1]
    factor = 2.0 / (features * epsilon)

    source_terms = lax.optimization_barrier(
        jnp.stack(
            [
                jnp.sum(jnp.square(sources.astype(jnp.float32)), 1) / features,
                log_source_mass,
            ]
        )
    )
    rows = targets.shape[0]
    everything = lax.all_to_all(
        jnp.broadcast_to(targets[None], (count,) + targets.shape), AXES, 0, 0, tiled=True
    ).reshape(count * rows, features)
    pots = lax.all_to_all(
        jnp.broadcast_to(target_potential[None, :, None], (count, rows, 128)), AXES, 0, 0, tiled=True
    ).reshape(count * rows, 128)

    width = targets.shape[0]
    vmem = pl.BlockSpec(memory_space=pltpu.VMEM)
    columns, source_potential = pl.pallas_call(
        functools.partial(tail, features, factor, width),
        out_shape=(
            jax.ShapeDtypeStruct((count, 2 * width), jnp.float32),
            jax.ShapeDtypeStruct((1, sources.shape[0]), jnp.float32),
        ),
        in_specs=[vmem] * 4,
        out_specs=(vmem, vmem),
        compiler_params=pltpu.CompilerParams(vmem_limit_bytes=24 * 1024 * 1024),
    )(sources, everything, pots, source_terms)
    source_potential = source_potential.reshape(-1)

    part = lax.all_to_all(columns, AXES, 0, 0, tiled=True)
    owned_max = jnp.max(part[:, :width], 0)
    owned_sum = jnp.sum(part[:, width:] * jnp.exp(part[:, :width] - owned_max[None, :]), 0)
    part = (owned_max, owned_sum)

    target_update = epsilon * (log_target_mass - (part[0] + jnp.log(part[1])))
    return (source_potential, target_update)


def solution(mesh):
    return jax.shard_map(
        per_device,
        mesh=mesh,
        in_specs=(
            P(AXES, None),
            P(AXES, None),
            P(AXES),
            P(AXES),
            P(AXES),
        ),
        out_specs=(P(AXES), P(AXES)),
        check_vma=False,
    )
```

```python
import functools

import jax
import jax.numpy as jnp
from jax import lax
from jax.sharding import PartitionSpec as P
from jax.experimental import pallas as pl
from jax.experimental.pallas import tpu as pltpu

epsilon = 0.05
AXES = ("group", "blk")


def tail(features, factor, width, src_ref, rows_ref, pots_ref, terms_ref, col_ref, pot_ref):
    block = rows = rows_ref[...]
    pots = pots_ref[...].astype(jnp.float32)
    offset = pots / epsilon - jnp.sum(jnp.square(rows.astype(jnp.float32)), 1, keepdims=True) / (
        features * epsilon
    )
    logits = lax.dot_general(
        rows, src_ref[...], (((1,), (1,)), ((), ())), preferred_element_type=jnp.float32
    ) * factor + offset
    row_max = jnp.max(logits, 0, keepdims=True)
    row_lse = row_max + jnp.log(jnp.sum(jnp.exp(logits - row_max), 0, keepdims=True))
    dual = terms_ref[1:2, :] - row_lse
    pot_ref[...] = epsilon * dual + terms_ref[0:1, :]
    column = logits - pots / epsilon + dual
    col_max = jnp.max(column, 1, keepdims=True)
    col_sum = jnp.sum(jnp.exp(column - col_max), 1, keepdims=True)
    diagonal = lax.broadcasted_iota(jnp.int32, (width, width), 0) == lax.broadcasted_iota(
        jnp.int32, (width, width), 1
    )
    for owner in range(block.shape[0] // width):
        first = owner * width
        for lanes, stat in ((0, col_max), (width, col_sum)):
            piece = jnp.where(diagonal, stat[first:first + width], 0.0)
            col_ref[owner:owner + 1, lanes:lanes + width] = jnp.sum(piece, 0, keepdims=True)


def per_device(sources, targets, target_potential, log_source_mass, log_target_mass):
    count = lax.axis_size("group") * lax.axis_size("blk")
    features = sources.shape[1]
    factor = 2.0 / (features * epsilon)

    source_terms = lax.optimization_barrier(
        jnp.stack(
            [
                jnp.sum(jnp.square(sources.astype(jnp.float32)), 1) / features,
                log_source_mass,
            ]
        )
    )
    rows = targets.shape[0]
    flat = rows * features
    spare = -(flat + rows) % 128
    chunk = jnp.concatenate(
        [targets.reshape(flat), target_potential, jnp.zeros((spare,), targets.dtype)]
    )
    everything = lax.all_to_all(
        jnp.broadcast_to(chunk[None], (count, chunk.shape[0])), AXES, 0, 0, tiled=True
    )
    pots = everything[:, flat:flat + rows].reshape(count * rows, 1)
    everything = everything[:, :flat].reshape(count * rows, features)

    width = targets.shape[0]
    vmem = pl.BlockSpec(memory_space=pltpu.VMEM)
    columns, source_potential = pl.pallas_call(
        functools.partial(tail, features, factor, width),
        out_shape=(
            jax.ShapeDtypeStruct((count, 2 * width), jnp.float32),
            jax.ShapeDtypeStruct((1, sources.shape[0]), jnp.float32),
        ),
        in_specs=[vmem] * 4,
        out_specs=(vmem, vmem),
        compiler_params=pltpu.CompilerParams(vmem_limit_bytes=24 * 1024 * 1024),
    )(sources, everything, pots, source_terms)
    source_potential = source_potential.reshape(-1)

    part = lax.all_to_all(columns, AXES, 0, 0, tiled=True)
    owned_max = jnp.max(part[:, :width], 0)
    owned_sum = jnp.sum(part[:, width:] * jnp.exp(part[:, :width] - owned_max[None, :]), 0)
    part = (owned_max, owned_sum)

    target_update = epsilon * (log_target_mass - (part[0] + jnp.log(part[1])))
    return (source_potential, target_update)


def solution(mesh):
    return jax.shard_map(
        per_device,
        mesh=mesh,
        in_specs=(
            P(AXES, None),
            P(AXES, None),
            P(AXES),
            P(AXES),
            P(AXES),
        ),
        out_specs=(P(AXES), P(AXES)),
        check_vma=False,
    )
```

```python
import functools

import jax
import jax.numpy as jnp
from jax import lax
from jax.sharding import PartitionSpec as P
from jax.experimental import pallas as pl
from jax.experimental.pallas import tpu as pltpu

epsilon = 0.05
AXES = ("group", "blk")


def tail(features, factor, width, src_ref, rows_ref, terms_ref, col_ref, pot_ref):
    block = rows_ref[...]
    rows = block[:, :features]
    pots = block[:, features:features + 1].astype(jnp.float32)
    offset = pots / epsilon - jnp.sum(jnp.square(rows.astype(jnp.float32)), 1, keepdims=True) / (
        features * epsilon
    )
    logits = lax.dot_general(
        rows, src_ref[...], (((1,), (1,)), ((), ())), preferred_element_type=jnp.float32
    ) * factor + offset
    row_max = jnp.max(logits, 0, keepdims=True)
    row_lse = row_max + jnp.log(jnp.sum(jnp.exp(logits - row_max), 0, keepdims=True))
    dual = terms_ref[1:2, :] - row_lse
    pot_ref[...] = epsilon * dual + terms_ref[0:1, :]
    column = logits - pots / epsilon + dual
    col_max = jnp.max(column, 1, keepdims=True)
    col_sum = jnp.sum(jnp.exp(column - col_max), 1, keepdims=True)
    targets_all = block.shape[0]
    r = lax.broadcasted_iota(jnp.int32, (targets_all, 2 * width), 0)
    c = lax.broadcasted_iota(jnp.int32, (targets_all, 2 * width), 1)
    spread = jnp.where(c == r % width, col_max, jnp.where(c == r % width + width, col_sum, 0.0))
    owners = lax.broadcasted_iota(jnp.int32, (targets_all // width, targets_all), 0)
    members = lax.broadcasted_iota(jnp.int32, (targets_all // width, targets_all), 1) // width
    gather = (owners == members).astype(jnp.float32)
    col_ref[...] = jnp.dot(
        gather, spread, precision=lax.Precision.HIGHEST, preferred_element_type=jnp.float32
    )

def per_device(sources, targets, target_potential, log_source_mass, log_target_mass):
    count = lax.axis_size("group") * lax.axis_size("blk")
    features = sources.shape[1]
    factor = 2.0 / (features * epsilon)

    lane = lax.broadcasted_iota(jnp.int32, (targets.shape[0], features + 128), 1)
    held = lax.optimization_barrier(
        jnp.where(
            lane < features,
            jnp.pad(targets, ((0, 0), (0, 128))),
            target_potential[:, None],
        )
    )
    source_terms = lax.optimization_barrier(
        jnp.stack(
            [
                jnp.sum(jnp.square(sources.astype(jnp.float32)), 1) / features,
                log_source_mass,
            ]
        )
    )
    everything = lax.all_to_all(
        jnp.broadcast_to(held[None], (count,) + held.shape), AXES, 0, 0, tiled=True
    ).reshape(count * held.shape[0], held.shape[1])

    width = targets.shape[0]
    vmem = pl.BlockSpec(memory_space=pltpu.VMEM)
    columns, source_potential = pl.pallas_call(
        functools.partial(tail, features, factor, width),
        out_shape=(
            jax.ShapeDtypeStruct((count, 2 * width), jnp.float32),
            jax.ShapeDtypeStruct((1, sources.shape[0]), jnp.float32),
        ),
        in_specs=[vmem] * 3,
        out_specs=(vmem, vmem),
        compiler_params=pltpu.CompilerParams(vmem_limit_bytes=24 * 1024 * 1024),
    )(sources, everything, source_terms)
    source_potential = source_potential.reshape(-1)

    part = lax.all_to_all(columns, AXES, 0, 0, tiled=True)
    owned_max = jnp.max(part[:, :width], 0)
    owned_sum = jnp.sum(part[:, width:] * jnp.exp(part[:, :width] - owned_max[None, :]), 0)
    part = (owned_max, owned_sum)

    target_update = epsilon * (log_target_mass - (part[0] + jnp.log(part[1])))
    return (source_potential, target_update)


def solution(mesh):
    return jax.shard_map(
        per_device,
        mesh=mesh,
        in_specs=(
            P(AXES, None),
            P(AXES, None),
            P(AXES),
            P(AXES),
            P(AXES),
        ),
        out_specs=(P(AXES), P(AXES)),
        check_vma=False,
    )
```

```python
import functools

import jax
import jax.numpy as jnp
from jax import lax
from jax.sharding import PartitionSpec as P
from jax.experimental import pallas as pl
from jax.experimental.pallas import tpu as pltpu

epsilon = 0.05
AXES = ("group", "blk")


def spread_out(features, rows_ref, pots_ref, out_ref):
    rows = rows_ref.shape[0]
    diagonal = lax.broadcasted_iota(jnp.int32, (rows, rows), 0) == lax.broadcasted_iota(
        jnp.int32, (rows, rows), 1
    )
    pots = pots_ref[...].astype(jnp.float32)
    column = jnp.sum(jnp.where(diagonal, pots, 0.0), 1, keepdims=True)
    lanes = jnp.broadcast_to(column, (rows, 128)).astype(out_ref.dtype)
    block = rows_ref[...]
    for k in range(out_ref.shape[0]):
        out_ref[k, :, 0:features] = block
        out_ref[k, :, features:features + 128] = lanes


def tail(features, factor, width, src_ref, rows_ref, terms_ref, col_ref, pot_ref):
    block = rows_ref[...]
    rows = block[:, :features]
    pots = block[:, features:features + 1].astype(jnp.float32)
    offset = pots / epsilon - jnp.sum(jnp.square(rows.astype(jnp.float32)), 1, keepdims=True) / (
        features * epsilon
    )
    logits = lax.dot_general(
        rows, src_ref[...], (((1,), (1,)), ((), ())), preferred_element_type=jnp.float32
    ) * factor + offset
    row_max = jnp.max(logits, 0, keepdims=True)
    row_lse = row_max + jnp.log(jnp.sum(jnp.exp(logits - row_max), 0, keepdims=True))
    dual = terms_ref[1:2, :] - row_lse
    pot_ref[...] = epsilon * dual + terms_ref[0:1, :]
    column = logits - pots / epsilon + dual
    col_max = jnp.max(column, 1, keepdims=True)
    col_sum = jnp.sum(jnp.exp(column - col_max), 1, keepdims=True)
    targets_all = block.shape[0]
    r = lax.broadcasted_iota(jnp.int32, (targets_all, 2 * width), 0)
    c = lax.broadcasted_iota(jnp.int32, (targets_all, 2 * width), 1)
    spread = jnp.where(c == r % width, col_max, jnp.where(c == r % width + width, col_sum, 0.0))
    owners = lax.broadcasted_iota(jnp.int32, (targets_all // width, targets_all), 0)
    members = lax.broadcasted_iota(jnp.int32, (targets_all // width, targets_all), 1) // width
    gather = (owners == members).astype(jnp.float32)
    col_ref[...] = jnp.dot(
        gather, spread, precision=lax.Precision.HIGHEST, preferred_element_type=jnp.float32
    )

def per_device(sources, targets, target_potential, log_source_mass, log_target_mass):
    count = lax.axis_size("group") * lax.axis_size("blk")
    features = sources.shape[1]
    factor = 2.0 / (features * epsilon)

    source_terms = lax.optimization_barrier(
        jnp.stack(
            [
                jnp.sum(jnp.square(sources.astype(jnp.float32)), 1) / features,
                log_source_mass,
            ]
        )
    )
    vmem = pl.BlockSpec(memory_space=pltpu.VMEM)
    outgoing = pl.pallas_call(
        functools.partial(spread_out, features),
        out_shape=jax.ShapeDtypeStruct((count, targets.shape[0], features + 128), targets.dtype),
        in_specs=[vmem] * 2,
        out_specs=vmem,
        compiler_params=pltpu.CompilerParams(vmem_limit_bytes=8 * 1024 * 1024),
    )(targets, target_potential.reshape(1, -1))
    everything = lax.all_to_all(outgoing, AXES, 0, 0, tiled=True).reshape(
        count * targets.shape[0], features + 128
    )

    width = targets.shape[0]
    columns, source_potential = pl.pallas_call(
        functools.partial(tail, features, factor, width),
        out_shape=(
            jax.ShapeDtypeStruct((count, 2 * width), jnp.float32),
            jax.ShapeDtypeStruct((1, sources.shape[0]), jnp.float32),
        ),
        in_specs=[vmem] * 3,
        out_specs=(vmem, vmem),
        compiler_params=pltpu.CompilerParams(vmem_limit_bytes=24 * 1024 * 1024),
    )(sources, everything, source_terms)
    source_potential = source_potential.reshape(-1)

    part = lax.all_to_all(columns, AXES, 0, 0, tiled=True)
    owned_max = jnp.max(part[:, :width], 0)
    owned_sum = jnp.sum(part[:, width:] * jnp.exp(part[:, :width] - owned_max[None, :]), 0)
    part = (owned_max, owned_sum)

    target_update = epsilon * (log_target_mass - (part[0] + jnp.log(part[1])))
    return (source_potential, target_update)


def solution(mesh):
    return jax.shard_map(
        per_device,
        mesh=mesh,
        in_specs=(
            P(AXES, None),
            P(AXES, None),
            P(AXES),
            P(AXES),
            P(AXES),
        ),
        out_specs=(P(AXES), P(AXES)),
        check_vma=False,
    )
```

```python
import functools

import jax
import jax.numpy as jnp
from jax import lax
from jax.sharding import PartitionSpec as P
from jax.experimental import pallas as pl
from jax.experimental.pallas import tpu as pltpu

epsilon = 0.05
AXES = ("group", "blk")


def tail(features, factor, width, src_ref, rows_ref, terms_ref, col_ref, pot_ref):
    block = rows_ref[...]
    rows = block[:, :features]
    pots = block[:, features:features + 1].astype(jnp.float32)
    offset = pots / epsilon - jnp.sum(jnp.square(rows.astype(jnp.float32)), 1, keepdims=True) / (
        features * epsilon
    )
    logits = jnp.dot(rows, src_ref[...], preferred_element_type=jnp.float32) * factor + offset
    row_max = jnp.max(logits, 0, keepdims=True)
    row_lse = row_max + jnp.log(jnp.sum(jnp.exp(logits - row_max), 0, keepdims=True))
    dual = terms_ref[1:2, :] - row_lse
    pot_ref[...] = epsilon * dual + terms_ref[0:1, :]
    column = logits - pots / epsilon + dual
    col_max = jnp.max(column, 1, keepdims=True)
    col_sum = jnp.sum(jnp.exp(column - col_max), 1, keepdims=True)
    targets_all = block.shape[0]
    r = lax.broadcasted_iota(jnp.int32, (targets_all, 2 * width), 0)
    c = lax.broadcasted_iota(jnp.int32, (targets_all, 2 * width), 1)
    spread = jnp.where(c == r % width, col_max, jnp.where(c == r % width + width, col_sum, 0.0))
    owners = lax.broadcasted_iota(jnp.int32, (targets_all // width, targets_all), 0)
    members = lax.broadcasted_iota(jnp.int32, (targets_all // width, targets_all), 1) // width
    gather = (owners == members).astype(jnp.float32)
    col_ref[...] = jnp.dot(
        gather, spread, precision=lax.Precision.HIGHEST, preferred_element_type=jnp.float32
    )

def per_device(sources, targets, target_potential, log_source_mass, log_target_mass):
    count = lax.axis_size("group") * lax.axis_size("blk")
    features = sources.shape[1]
    factor = 2.0 / (features * epsilon)

    lane = lax.broadcasted_iota(jnp.int32, (targets.shape[0], features + 128), 1)
    held = lax.optimization_barrier(
        jnp.where(
            lane < features,
            jnp.pad(targets, ((0, 0), (0, 128))),
            target_potential[:, None],
        )
    )
    source_terms = lax.optimization_barrier(
        jnp.stack(
            [
                jnp.sum(jnp.square(sources.astype(jnp.float32)), 1) / features,
                log_source_mass,
            ]
        )
    )
    everything = lax.all_to_all(
        jnp.broadcast_to(held[None], (count,) + held.shape), AXES, 0, 0, tiled=True
    ).reshape(count * held.shape[0], held.shape[1])

    width = targets.shape[0]
    vmem = pl.BlockSpec(memory_space=pltpu.VMEM)
    columns, source_potential = pl.pallas_call(
        functools.partial(tail, features, factor, width),
        out_shape=(
            jax.ShapeDtypeStruct((count, 2 * width), jnp.float32),
            jax.ShapeDtypeStruct((1, sources.shape[0]), jnp.float32),
        ),
        in_specs=[vmem] * 3,
        out_specs=(vmem, vmem),
        compiler_params=pltpu.CompilerParams(vmem_limit_bytes=24 * 1024 * 1024),
    )(sources.T, everything, source_terms)
    source_potential = source_potential.reshape(-1)

    part = lax.all_to_all(columns, AXES, 0, 0, tiled=True)
    owned_max = jnp.max(part[:, :width], 0)
    owned_sum = jnp.sum(part[:, width:] * jnp.exp(part[:, :width] - owned_max[None, :]), 0)
    part = (owned_max, owned_sum)

    target_update = epsilon * (log_target_mass - (part[0] + jnp.log(part[1])))
    return (source_potential, target_update)


def solution(mesh):
    return jax.shard_map(
        per_device,
        mesh=mesh,
        in_specs=(
            P(AXES, None),
            P(AXES, None),
            P(AXES),
            P(AXES),
            P(AXES),
        ),
        out_specs=(P(AXES), P(AXES)),
        check_vma=False,
    )
```

```python
import functools

import jax
import jax.numpy as jnp
from jax import lax
from jax.sharding import PartitionSpec as P
from jax.experimental import pallas as pl
from jax.experimental.pallas import tpu as pltpu

epsilon = 0.05
AXES = ("group", "blk")


def tail(features, factor, width, src_ref, rows_ref, terms_ref, col_ref, dual_ref):
    block = rows_ref[...]
    rows = block[:, :features]
    pots = block[:, features:features + 1].astype(jnp.float32)
    offset = pots / epsilon - jnp.sum(jnp.square(rows.astype(jnp.float32)), 1, keepdims=True) / (
        features * epsilon
    )
    logits = jnp.dot(rows, src_ref[...], preferred_element_type=jnp.float32) * factor + offset
    row_max = jnp.max(logits, 0, keepdims=True)
    row_lse = row_max + jnp.log(jnp.sum(jnp.exp(logits - row_max), 0, keepdims=True))
    dual = terms_ref[1:2, :] - row_lse
    dual_ref[...] = dual
    column = logits - pots / epsilon + dual
    col_max = jnp.max(column, 1, keepdims=True)
    col_sum = jnp.sum(jnp.exp(column - col_max), 1, keepdims=True)
    targets_all = block.shape[0]
    r = lax.broadcasted_iota(jnp.int32, (targets_all, 2 * width), 0)
    c = lax.broadcasted_iota(jnp.int32, (targets_all, 2 * width), 1)
    spread = jnp.where(c == r % width, col_max, jnp.where(c == r % width + width, col_sum, 0.0))
    owners = lax.broadcasted_iota(jnp.int32, (targets_all // width, targets_all), 0)
    members = lax.broadcasted_iota(jnp.int32, (targets_all // width, targets_all), 1) // width
    gather = (owners == members).astype(jnp.float32)
    col_ref[...] = jnp.dot(
        gather, spread, precision=lax.Precision.HIGHEST, preferred_element_type=jnp.float32
    )

def per_device(sources, targets, target_potential, log_source_mass, log_target_mass):
    count = lax.axis_size("group") * lax.axis_size("blk")
    features = sources.shape[1]
    factor = 2.0 / (features * epsilon)

    lane = lax.broadcasted_iota(jnp.int32, (targets.shape[0], features + 128), 1)
    held = lax.optimization_barrier(
        jnp.where(
            lane < features,
            jnp.pad(targets, ((0, 0), (0, 128))),
            target_potential[:, None],
        )
    )
    source_terms = lax.optimization_barrier(
        jnp.stack(
            [
                jnp.sum(jnp.square(sources.astype(jnp.float32)), 1) / features,
                log_source_mass,
            ]
        )
    )
    everything = lax.all_to_all(
        jnp.broadcast_to(held[None], (count,) + held.shape), AXES, 0, 0, tiled=True
    ).reshape(count * held.shape[0], held.shape[1])

    width = targets.shape[0]
    vmem = pl.BlockSpec(memory_space=pltpu.VMEM)
    columns, source_dual = pl.pallas_call(
        functools.partial(tail, features, factor, width),
        out_shape=(
            jax.ShapeDtypeStruct((count, 2 * width), jnp.float32),
            jax.ShapeDtypeStruct((1, sources.shape[0]), jnp.float32),
        ),
        in_specs=[vmem] * 3,
        out_specs=(vmem, vmem),
        compiler_params=pltpu.CompilerParams(vmem_limit_bytes=24 * 1024 * 1024),
    )(sources.T, everything, source_terms)
    source_potential = epsilon * source_dual.reshape(-1) + source_terms[0]

    part = lax.all_to_all(columns, AXES, 0, 0, tiled=True)
    owned_max = jnp.max(part[:, :width], 0)
    owned_sum = jnp.sum(part[:, width:] * jnp.exp(part[:, :width] - owned_max[None, :]), 0)
    part = (owned_max, owned_sum)

    target_update = epsilon * (log_target_mass - (part[0] + jnp.log(part[1])))
    return (source_potential, target_update)


def solution(mesh):
    return jax.shard_map(
        per_device,
        mesh=mesh,
        in_specs=(
            P(AXES, None),
            P(AXES, None),
            P(AXES),
            P(AXES),
            P(AXES),
        ),
        out_specs=(P(AXES), P(AXES)),
        check_vma=False,
    )
```

```python
import functools

import jax
import jax.numpy as jnp
from jax import lax
from jax.sharding import PartitionSpec as P
from jax.experimental import pallas as pl
from jax.experimental.pallas import tpu as pltpu

epsilon = 0.05
AXES = ("group", "blk")


def tail(features, factor, width, src_ref, rows_ref, terms_ref, col_ref, pot_ref):
    block = rows_ref[...]
    rows = block[:, :features]
    pots = block[:, features:features + 1].astype(jnp.float32)
    offset = pots / epsilon - jnp.sum(jnp.square(rows.astype(jnp.float32)), 1, keepdims=True) / (
        features * epsilon
    )
    logits = jnp.dot(rows, src_ref[...], preferred_element_type=jnp.float32) * factor + offset
    row_max = jnp.max(logits, 0, keepdims=True)
    row_lse = row_max + jnp.log(jnp.sum(jnp.exp(logits - row_max), 0, keepdims=True))
    dual = terms_ref[1:2, :] - row_lse
    pot_ref[...] = epsilon * dual + terms_ref[0:1, :]
    column = logits - pots / epsilon + dual
    col_max = jnp.max(column, 1, keepdims=True)
    col_sum = jnp.sum(jnp.exp(column - col_max), 1, keepdims=True)
    targets_all = block.shape[0]
    r = lax.broadcasted_iota(jnp.int32, (targets_all, 2 * width), 0)
    c = lax.broadcasted_iota(jnp.int32, (targets_all, 2 * width), 1)
    spread = jnp.where(c == r % width, col_max, jnp.where(c == r % width + width, col_sum, 0.0))
    owners = lax.broadcasted_iota(jnp.int32, (targets_all // width, targets_all), 0)
    members = lax.broadcasted_iota(jnp.int32, (targets_all // width, targets_all), 1) // width
    gather = (owners == members).astype(jnp.float32)
    col_ref[...] = jnp.dot(
        gather, spread, precision=lax.Precision.HIGHEST, preferred_element_type=jnp.float32
    )

def per_device(sources, targets, target_potential, log_source_mass, log_target_mass):
    count = lax.axis_size("group") * lax.axis_size("blk")
    features = sources.shape[1]
    factor = 2.0 / (features * epsilon)

    lane = lax.broadcasted_iota(jnp.int32, (targets.shape[0], features + 128), 1)
    held = lax.optimization_barrier(
        jnp.where(
            lane < features,
            jnp.pad(targets, ((0, 0), (0, 128))),
            target_potential[:, None],
        )
    )
    source_terms = lax.optimization_barrier(
        jnp.stack(
            [
                jnp.sum(jnp.square(sources.astype(jnp.float32)), 1) / features,
                log_source_mass,
            ]
        )
    )
    everything = lax.all_to_all(
        jnp.broadcast_to(held[None], (count,) + held.shape), AXES[::-1], 0, 0, tiled=True
    ).reshape(count * held.shape[0], held.shape[1])

    width = targets.shape[0]
    vmem = pl.BlockSpec(memory_space=pltpu.VMEM)
    columns, source_potential = pl.pallas_call(
        functools.partial(tail, features, factor, width),
        out_shape=(
            jax.ShapeDtypeStruct((count, 2 * width), jnp.float32),
            jax.ShapeDtypeStruct((1, sources.shape[0]), jnp.float32),
        ),
        in_specs=[vmem] * 3,
        out_specs=(vmem, vmem),
        compiler_params=pltpu.CompilerParams(vmem_limit_bytes=24 * 1024 * 1024),
    )(sources.T, everything, source_terms)
    source_potential = source_potential.reshape(-1)

    part = lax.all_to_all(columns, AXES[::-1], 0, 0, tiled=True)
    owned_max = jnp.max(part[:, :width], 0)
    owned_sum = jnp.sum(part[:, width:] * jnp.exp(part[:, :width] - owned_max[None, :]), 0)
    part = (owned_max, owned_sum)

    target_update = epsilon * (log_target_mass - (part[0] + jnp.log(part[1])))
    return (source_potential, target_update)


def solution(mesh):
    return jax.shard_map(
        per_device,
        mesh=mesh,
        in_specs=(
            P(AXES, None),
            P(AXES, None),
            P(AXES),
            P(AXES),
            P(AXES),
        ),
        out_specs=(P(AXES), P(AXES)),
        check_vma=False,
    )
```

```python
import functools

import jax
import jax.numpy as jnp
from jax import lax
from jax.sharding import PartitionSpec as P
from jax.experimental import pallas as pl
from jax.experimental.pallas import tpu as pltpu

epsilon = 0.05
AXES = ("group", "blk")


def tail(features, factor, width, src_ref, rows_ref, terms_ref, col_ref, pot_ref):
    block = rows_ref[...]
    rows = block[:, :features]
    pots = block[:, features:features + 1].astype(jnp.float32)
    offset = pots / epsilon - jnp.sum(jnp.square(rows.astype(jnp.float32)), 1, keepdims=True) / (
        features * epsilon
    )
    logits = jnp.dot(rows, src_ref[...], preferred_element_type=jnp.float32) * factor + offset
    row_max = jnp.max(logits, 0, keepdims=True)
    row_lse = row_max + jnp.log(jnp.sum(jnp.exp(logits - row_max), 0, keepdims=True))
    dual = terms_ref[1:2, :] - row_lse
    pot_ref[...] = epsilon * dual + terms_ref[0:1, :]
    column = logits - pots / epsilon + dual
    col_max = jnp.max(column, 1, keepdims=True)
    ones = jnp.ones((column.shape[1], 128), jnp.float32)
    col_sum = jnp.dot(
        jnp.exp(column - col_max), ones, precision=lax.Precision.HIGHEST,
        preferred_element_type=jnp.float32,
    )[:, 0:1]
    targets_all = block.shape[0]
    r = lax.broadcasted_iota(jnp.int32, (targets_all, 2 * width), 0)
    c = lax.broadcasted_iota(jnp.int32, (targets_all, 2 * width), 1)
    spread = jnp.where(c == r % width, col_max, jnp.where(c == r % width + width, col_sum, 0.0))
    owners = lax.broadcasted_iota(jnp.int32, (targets_all // width, targets_all), 0)
    members = lax.broadcasted_iota(jnp.int32, (targets_all // width, targets_all), 1) // width
    gather = (owners == members).astype(jnp.float32)
    col_ref[...] = jnp.dot(
        gather, spread, precision=lax.Precision.HIGHEST, preferred_element_type=jnp.float32
    )

def per_device(sources, targets, target_potential, log_source_mass, log_target_mass):
    count = lax.axis_size("group") * lax.axis_size("blk")
    features = sources.shape[1]
    factor = 2.0 / (features * epsilon)

    lane = lax.broadcasted_iota(jnp.int32, (targets.shape[0], features + 128), 1)
    held = lax.optimization_barrier(
        jnp.where(
            lane < features,
            jnp.pad(targets, ((0, 0), (0, 128))),
            target_potential[:, None],
        )
    )
    source_terms = lax.optimization_barrier(
        jnp.stack(
            [
                jnp.sum(jnp.square(sources.astype(jnp.float32)), 1) / features,
                log_source_mass,
            ]
        )
    )
    everything = lax.all_to_all(
        jnp.broadcast_to(held[None], (count,) + held.shape), AXES, 0, 0, tiled=True
    ).reshape(count * held.shape[0], held.shape[1])

    width = targets.shape[0]
    vmem = pl.BlockSpec(memory_space=pltpu.VMEM)
    columns, source_potential = pl.pallas_call(
        functools.partial(tail, features, factor, width),
        out_shape=(
            jax.ShapeDtypeStruct((count, 2 * width), jnp.float32),
            jax.ShapeDtypeStruct((1, sources.shape[0]), jnp.float32),
        ),
        in_specs=[vmem] * 3,
        out_specs=(vmem, vmem),
        compiler_params=pltpu.CompilerParams(vmem_limit_bytes=24 * 1024 * 1024),
    )(sources.T, everything, source_terms)
    source_potential = source_potential.reshape(-1)

    part = lax.all_to_all(columns, AXES, 0, 0, tiled=True)
    owned_max = jnp.max(part[:, :width], 0)
    owned_sum = jnp.sum(part[:, width:] * jnp.exp(part[:, :width] - owned_max[None, :]), 0)
    part = (owned_max, owned_sum)

    target_update = epsilon * (log_target_mass - (part[0] + jnp.log(part[1])))
    return (source_potential, target_update)


def solution(mesh):
    return jax.shard_map(
        per_device,
        mesh=mesh,
        in_specs=(
            P(AXES, None),
            P(AXES, None),
            P(AXES),
            P(AXES),
            P(AXES),
        ),
        out_specs=(P(AXES), P(AXES)),
        check_vma=False,
    )
```

```python
import functools

import jax
import jax.numpy as jnp
from jax import lax
from jax.sharding import PartitionSpec as P
from jax.experimental import pallas as pl
from jax.experimental.pallas import tpu as pltpu

epsilon = 0.05
AXES = ("group", "blk")


def tail(features, factor, width, src_ref, rows_ref, terms_ref, col_ref, pot_ref):
    block = rows_ref[...]
    rows = block[:, :features]
    pots = block[:, features:features + 1].astype(jnp.float32)
    offset = pots / epsilon - jnp.sum(jnp.square(rows.astype(jnp.float32)), 1, keepdims=True) / (
        features * epsilon
    )
    logits = jnp.dot(rows, src_ref[...], preferred_element_type=jnp.float32) * factor + offset
    row_max = jnp.max(logits, 0, keepdims=True)
    row_lse = row_max + jnp.log(jnp.sum(jnp.exp(logits - row_max), 0, keepdims=True))
    dual = terms_ref[1:2, :] - row_lse
    pot_ref[...] = epsilon * dual + terms_ref[0:1, :]
    column = logits - pots / epsilon + dual
    col_max = jnp.max(column, 1, keepdims=True)
    col_sum = jnp.sum(jnp.exp(column - col_max), 1, keepdims=True)
    targets_all = block.shape[0]
    r = lax.broadcasted_iota(jnp.int32, (targets_all, 2 * width), 0)
    c = lax.broadcasted_iota(jnp.int32, (targets_all, 2 * width), 1)
    spread = jnp.where(c == r % width, col_max, jnp.where(c == r % width + width, col_sum, 0.0))
    owners = lax.broadcasted_iota(jnp.int32, (targets_all // width, targets_all), 0)
    members = lax.broadcasted_iota(jnp.int32, (targets_all // width, targets_all), 1) // width
    gather = (owners == members).astype(jnp.float32)
    col_ref[...] = jnp.dot(
        gather, spread, precision=lax.Precision.HIGH, preferred_element_type=jnp.float32
    )

def per_device(sources, targets, target_potential, log_source_mass, log_target_mass):
    count = lax.axis_size("group") * lax.axis_size("blk")
    features = sources.shape[1]
    factor = 2.0 / (features * epsilon)

    lane = lax.broadcasted_iota(jnp.int32, (targets.shape[0], features + 128), 1)
    held = lax.optimization_barrier(
        jnp.where(
            lane < features,
            jnp.pad(targets, ((0, 0), (0, 128))),
            target_potential[:, None],
        )
    )
    source_terms = lax.optimization_barrier(
        jnp.stack(
            [
                jnp.sum(jnp.square(sources.astype(jnp.float32)), 1) / features,
                log_source_mass,
            ]
        )
    )
    everything = lax.all_to_all(
        jnp.broadcast_to(held[None], (count,) + held.shape), AXES, 0, 0, tiled=True
    ).reshape(count * held.shape[0], held.shape[1])

    width = targets.shape[0]
    vmem = pl.BlockSpec(memory_space=pltpu.VMEM)
    columns, source_potential = pl.pallas_call(
        functools.partial(tail, features, factor, width),
        out_shape=(
            jax.ShapeDtypeStruct((count, 2 * width), jnp.float32),
            jax.ShapeDtypeStruct((1, sources.shape[0]), jnp.float32),
        ),
        in_specs=[vmem] * 3,
        out_specs=(vmem, vmem),
        compiler_params=pltpu.CompilerParams(vmem_limit_bytes=24 * 1024 * 1024),
    )(sources.T, everything, source_terms)
    source_potential = source_potential.reshape(-1)

    part = lax.all_to_all(columns, AXES, 0, 0, tiled=True)
    owned_max = jnp.max(part[:, :width], 0)
    owned_sum = jnp.sum(part[:, width:] * jnp.exp(part[:, :width] - owned_max[None, :]), 0)
    part = (owned_max, owned_sum)

    target_update = epsilon * (log_target_mass - (part[0] + jnp.log(part[1])))
    return (source_potential, target_update)


def solution(mesh):
    return jax.shard_map(
        per_device,
        mesh=mesh,
        in_specs=(
            P(AXES, None),
            P(AXES, None),
            P(AXES),
            P(AXES),
            P(AXES),
        ),
        out_specs=(P(AXES), P(AXES)),
        check_vma=False,
    )
```
